32 devices in a mesh: groups: 2 (over y), owner: 4 (over x, core), loop: 4 (over z).
Axes of the slice: x: 2, y: 2, z: 4, core: 2. Of those that a mesh axis runs over, the one named last changes fastest.
Arguments:
- emb: bfloat16 [8192, 1024], P(('groups', 'owner', 'loop')), parts along dimension 0, may hold values from -30 to 30
- row_owner: int32 [8192], P(('groups', 'owner', 'loop')), parts along dimension 0, may hold values from 0 to 3, as said below
- row_sub: int32 [8192], P(('groups', 'owner', 'loop')), parts along dimension 0, may hold values from 0 to 15, as said below
- cand: int32 [64, 32], P('groups'), parts along dimension 0, may hold values from 0 to 1, as said below
Outputs:
- dedup: bfloat16 [8192, 1024], P(('groups', 'owner', 'loop')), parts along dimension 0
The draws below stay inside these ranges and needn't reach their ends.
There are 2 independent parts, one for each index of `groups`. The reference program is written for one: setup_inputs(seed, part) draws one part's arguments, and reference() takes and returns one part's arrays. A program takes and returns all parts, laid end to end along the dimension named above; each array names one. Nothing has to cross between parts.
Inputs may be any that keep to these rules, and one draw needn't show every extreme that they name: `row_owner`: among the documents of one device no owner appears more than 128 times, and on every device some owner appears exactly 128 times. Documents 2k and 2k + 1 have the same owner and cluster. Documents 2k and 2k + 1 have the same cluster. Among the documents of one device with one owner, no more than 32 have a row_sub of one value modulo 4, and on every device some owner and residue have exactly 32. cand is 1 on its diagonal.
All inputs are finite; a program needn't handle non-finite values.
Results may differ from the reference program's by a relative error of at most 0.0017.
Values may be sent and summed in bfloat16 or wider, within the bound.
No kernel may reach another device: no remote copies, remote signals or barrier semaphores. Data moves between devices by JAX's collectives and lax.ppermute only.
A program may use at most 64 MiB of HBM per device.

```python
import jax
import jax.numpy as jnp
from jax import lax

D = 1024
ROWS_DEV = 256
BLOCK = 128
SUB = 16
ROWS = 4096
NBLOCKS = 32
CAP = 128
N_OWNER = 4
N_LOOP = 4


def draw_emb(key, part):
    first = jax.random.fold_in(jax.random.fold_in(key, 11), 0)
    result = jnp.clip(jax.random.normal(first, (ROWS, D), jnp.float32), -6.0, 6.0)
    return result.astype(jnp.bfloat16)


def pair_owners(key):
    first, second, third, fourth = jax.random.split(jax.random.fold_in(key, 23), 4)
    devices = ROWS // ROWS_DEV
    half_rows = ROWS_DEV // 2
    per_owner = ROWS_DEV // N_OWNER
    entries = N_OWNER * per_owner
    popular = jax.random.randint(first, (N_OWNER,), 0, 4)
    hottest = jax.random.randint(second, (devices,), 0, N_OWNER)
    entry_owner = jnp.arange(entries, dtype=jnp.int32) // per_owner
    noise = jax.random.randint(third, (devices, entries), 0, 65536)
    score = popular[entry_owner][None, :] * 65536 + noise
    score = score + (entry_owner[None, :] == hottest[:, None]).astype(jnp.int32) * (4 * 65536)
    score = score * entries + jnp.arange(entries, dtype=jnp.int32)[None, :]
    picked = lax.top_k(score, half_rows)[1]
    owners = entry_owner[picked]
    shuffle = jax.random.randint(fourth, (devices, half_rows), 0, 65536) * half_rows + jnp.arange(half_rows, dtype=jnp.int32)[None, :]
    order = jnp.argsort(shuffle, axis=1)
    return jnp.take_along_axis(owners, order, axis=1).astype(jnp.int32)


def draw_row_owner(key, part):
    owners = pair_owners(key)
    return jnp.repeat(owners, 2, axis=1).reshape(ROWS).astype(jnp.int32)


def draw_row_sub(key, part):
    owners = pair_owners(key)
    devices = ROWS // ROWS_DEV
    half_rows = ROWS_DEV // 2
    first, second = jax.random.split(jax.random.fold_in(key, 37), 2)
    slot_pairs = max(2, CAP // N_LOOP) // 2
    onehot = (owners[:, :, None] == jnp.arange(N_OWNER, dtype=jnp.int32)[None, None, :]).astype(jnp.int32)
    earlier = jnp.cumsum(onehot, axis=1) - onehot
    ordinal = jnp.sum(earlier * onehot, axis=2)
    offsets = jax.random.randint(first, (devices, N_OWNER), 0, N_LOOP)
    offset = jnp.take_along_axis(offsets, owners, axis=1)
    residue = (ordinal // slot_pairs + offset) % N_LOOP
    upper = jax.random.randint(second, (devices, half_rows), 0, SUB // N_LOOP)
    subs = residue + N_LOOP * upper
    return jnp.repeat(subs, 2, axis=1).reshape(ROWS).astype(jnp.int32)


def draw_cand(key, part):
    table = jax.random.randint(jax.random.fold_in(key, 53), (NBLOCKS, NBLOCKS), 0, 2)
    diagonal = jnp.arange(NBLOCKS)[:, None] == jnp.arange(NBLOCKS)[None, :]
    return jnp.where(diagonal, 1, table).astype(jnp.int32)


def setup_inputs(seed: int = 0, part: int = 0) -> dict:
    seeds = jax.random.split(jax.random.key(seed), 5)
    own_keys = jax.random.split(jax.random.fold_in(seeds[4], part), 5)
    emb = draw_emb(jax.random.fold_in(jax.random.fold_in(seeds[4], part), 71), part)
    row_owner = draw_row_owner(jax.random.fold_in(jax.random.fold_in(seeds[4], part), 71), part)
    row_sub = draw_row_sub(jax.random.fold_in(jax.random.fold_in(seeds[4], part), 71), part)
    cand = draw_cand(jax.random.fold_in(jax.random.fold_in(seeds[4], part), 71), part)
    return {"emb": emb, "row_owner": row_owner, "row_sub": row_sub, "cand": cand}


def reference(emb, row_owner, row_sub, cand):
    total_rows = emb.shape[0]
    width = emb.shape[1]
    scale = 4.0 / width
    cluster = (row_owner * SUB + row_sub).astype(jnp.int32)
    row_index = jnp.arange(total_rows, dtype=jnp.int32)
    blocks = (row_index // BLOCK).astype(jnp.int32)
    query_rows = min(512, total_rows)

    def one_block(start):
        start = start.astype(jnp.int32)
        queries = lax.dynamic_slice_in_dim(emb, start, query_rows, 0)
        query_cluster = lax.dynamic_slice_in_dim(cluster, start, query_rows, 0)
        query_block = lax.dynamic_slice_in_dim(blocks, start, query_rows, 0)
        query_index = lax.dynamic_slice_in_dim(row_index, start, query_rows, 0)
        scores = scale * jnp.dot(queries, emb.T, preferred_element_type=jnp.float32)
        near = jnp.take(cand, query_block, axis=0)[:, blocks] > 0
        allowed = (query_index[:, None] == row_index[None, :]) | ((query_cluster[:, None] == cluster[None, :]) & near)
        top = jnp.max(jnp.where(allowed, scores, jnp.float32(-1e30)), axis=1)
        weights = jnp.where(allowed, jnp.exp(scores - top[:, None]), jnp.float32(0.0))
        total = jnp.sum(weights, axis=1)
        summed = jnp.dot(weights.astype(jnp.bfloat16), emb, preferred_element_type=jnp.float32)
        return (summed / total[:, None]).astype(jnp.bfloat16)

    starts = jnp.arange(total_rows // query_rows, dtype=jnp.int32) * query_rows
    result = lax.map(one_block, starts)
    return result.reshape(total_rows, width)
```

```python
import jax
import jax.numpy as jnp
from jax import lax
from jax.sharding import PartitionSpec as P

BLOCK = 128
SUB = 16


def route(row_owner, row_sub, loop_count, capacity):
    devices = lax.axis_size("owner") * loop_count
    dest = row_owner * loop_count + row_sub % loop_count
    onehot = (dest[:, None] == jnp.arange(devices, dtype=jnp.int32)[None, :]).astype(jnp.bfloat16)
    rows = row_owner.shape[0]
    lower = (
        jnp.arange(rows, dtype=jnp.int32)[:, None] > jnp.arange(rows, dtype=jnp.int32)[None, :]
    ).astype(jnp.bfloat16)
    earlier = jnp.dot(lower, onehot, preferred_element_type=jnp.float32)
    within = jnp.sum(earlier * onehot.astype(jnp.float32), axis=1).astype(jnp.int32)
    return dest * capacity + within


def attend(keys, near, sub):
    slots = keys.shape[0]
    scale = 4.0 / keys.shape[1]
    scores = scale * lax.dot_general(
        keys, keys, (((1,), (1,)), ((), ())), preferred_element_type=jnp.float32
    )
    index = jnp.arange(slots, dtype=jnp.int32)
    same = (index[:, None] == index[None, :]) | (
        (sub[:, None] == sub[None, :]) & near
    )
    top = jnp.max(jnp.where(same, scores, jnp.float32(-1e30)), axis=1)
    weights = jnp.where(same, jnp.exp(scores - top[:, None]), jnp.float32(0.0))
    total = jnp.sum(weights, axis=1)
    summed = jnp.dot(weights.astype(jnp.bfloat16), keys, preferred_element_type=jnp.float32)
    return (summed / total[:, None]).astype(jnp.bfloat16)


def body(emb, row_owner, row_sub, cand):
    rows = emb.shape[0]
    owner_count = lax.axis_size("owner")
    loop_count = lax.axis_size("loop")
    devices = owner_count * loop_count
    capacity = 2 * rows // owner_count // loop_count
    slots = devices * capacity
    local_blocks = rows // BLOCK
    axes = ("owner", "loop")

    slot_of_row = route(row_owner, row_sub, loop_count, capacity)
    placing = (jnp.arange(slots, dtype=jnp.int32)[:, None] == slot_of_row[None, :]).astype(
        jnp.bfloat16
    )
    send_emb = jnp.dot(placing, emb, preferred_element_type=jnp.float32).astype(jnp.bfloat16)
    row_labels = jnp.stack(
        [jnp.arange(rows, dtype=jnp.int32) // BLOCK + 1, row_sub + 1], axis=1
    ).astype(jnp.bfloat16)
    send_labels = jnp.dot(placing, row_labels, preferred_element_type=jnp.float32).astype(
        jnp.int32
    )
    held_emb = lax.all_to_all(send_emb, axes, split_axis=0, concat_axis=0, tiled=True)
    held_labels = lax.all_to_all(send_labels, axes, split_axis=0, concat_axis=0, tiled=True)

    index = jnp.arange(slots, dtype=jnp.int32)
    present = held_labels[:, 0] > 0
    source = index // capacity
    global_block = source * local_blocks + held_labels[:, 0] - 1
    global_block = jnp.where(present, global_block, 0)
    sub = jnp.where(present, held_labels[:, 1] - 1, -1 - index)
    block_count = cand.shape[1]
    block_onehot = (
        global_block[:, None] == jnp.arange(block_count, dtype=jnp.int32)[None, :]
    ).astype(jnp.bfloat16)
    cand_rows = jnp.dot(block_onehot, cand.astype(jnp.bfloat16), preferred_element_type=jnp.float32)
    near = (
        lax.dot_general(
            cand_rows.astype(jnp.bfloat16),
            block_onehot,
            (((1,), (1,)), ((), ())),
            preferred_element_type=jnp.float32,
        )
        > 0.5
    )
    averaged = attend(held_emb, near, sub)
    returned = lax.all_to_all(averaged, axes, split_axis=0, concat_axis=0, tiled=True)
    result = lax.dot_general(
        placing, returned, (((0,), (0,)), ((), ())), preferred_element_type=jnp.float32
    )
    return result.astype(jnp.bfloat16)


def solution(mesh):
    return jax.shard_map(
        body,
        mesh=mesh,
        in_specs=(
            P(("groups", "owner", "loop"), None),
            P(("groups", "owner", "loop")),
            P(("groups", "owner", "loop")),
            P("groups", None),
        ),
        out_specs=P(("groups", "owner", "loop"), None),
        check_vma=False,
    )
```

```python
import jax
import jax.numpy as jnp
from jax import lax
from jax.sharding import PartitionSpec as P

BLOCK = 128
SUB = 16


def route(row_owner, row_sub, loop_count, capacity):
    devices = lax.axis_size("owner") * loop_count
    dest = row_owner * loop_count + row_sub % loop_count
    onehot = (dest[:, None] == jnp.arange(devices, dtype=jnp.int32)[None, :]).astype(jnp.bfloat16)
    rows = row_owner.shape[0]
    lower = (
        jnp.arange(rows, dtype=jnp.int32)[:, None] > jnp.arange(rows, dtype=jnp.int32)[None, :]
    ).astype(jnp.bfloat16)
    earlier = jnp.dot(lower, onehot, preferred_element_type=jnp.float32)
    within = jnp.sum(earlier * onehot.astype(jnp.float32), axis=1).astype(jnp.int32)
    return dest * capacity + within


def arrivals(row_owner, row_sub, axes, loop_count, capacity):
    rows = row_owner.shape[0]
    packed = (row_owner * loop_count + row_sub % loop_count) * 1024 + row_sub
    every = lax.all_gather(packed, axes, axis=0, tiled=False)
    sources = every.shape[0]
    me = lax.axis_index("owner") * loop_count + lax.axis_index("loop")
    mine = every // 1024 == me
    upper = (
        jnp.arange(rows, dtype=jnp.int32)[:, None] < jnp.arange(rows, dtype=jnp.int32)[None, :]
    ).astype(jnp.bfloat16)
    within = jnp.dot(mine.astype(jnp.bfloat16), upper, preferred_element_type=jnp.float32)
    within = within.astype(jnp.int32)
    match = mine[:, None, :] & (
        within[:, None, :] == jnp.arange(capacity, dtype=jnp.int32)[None, :, None]
    )
    local_block = (jnp.arange(rows, dtype=jnp.int32) // BLOCK)[None, None, :]
    present = jnp.any(match, axis=2).reshape(sources * capacity)
    held_block = jnp.sum(jnp.where(match, local_block, 0), axis=2).reshape(sources * capacity)
    held_sub = jnp.sum(jnp.where(match, every[:, None, :] % 1024, 0), axis=2)
    held_sub = held_sub.reshape(sources * capacity)
    index = jnp.arange(sources * capacity, dtype=jnp.int32)
    return held_block, jnp.where(present, held_sub, -1 - index)


def attend(keys, near, sub):
    slots = keys.shape[0]
    scale = 4.0 / keys.shape[1]
    scores = scale * lax.dot_general(
        keys, keys, (((1,), (1,)), ((), ())), preferred_element_type=jnp.float32
    )
    index = jnp.arange(slots, dtype=jnp.int32)
    same = (index[:, None] == index[None, :]) | (
        (sub[:, None] == sub[None, :]) & near
    )
    top = jnp.max(jnp.where(same, scores, jnp.float32(-1e30)), axis=1)
    weights = jnp.where(same, jnp.exp(scores - top[:, None]), jnp.float32(0.0))
    total = jnp.sum(weights, axis=1)
    summed = jnp.dot(weights.astype(jnp.bfloat16), keys, preferred_element_type=jnp.float32)
    return (summed / total[:, None]).astype(jnp.bfloat16)


def body(emb, row_owner, row_sub, cand):
    rows = emb.shape[0]
    owner_count = lax.axis_size("owner")
    loop_count = lax.axis_size("loop")
    devices = owner_count * loop_count
    capacity = 2 * rows // owner_count // loop_count
    slots = devices * capacity
    local_blocks = rows // BLOCK
    axes = ("owner", "loop")

    slot_of_row = route(row_owner, row_sub, loop_count, capacity)
    placing = (jnp.arange(slots, dtype=jnp.int32)[:, None] == slot_of_row[None, :]).astype(
        jnp.bfloat16
    )
    send_emb = jnp.dot(placing, emb, preferred_element_type=jnp.float32).astype(jnp.bfloat16)
    held_emb = lax.all_to_all(send_emb, axes, split_axis=0, concat_axis=0, tiled=True)

    held_block, sub = arrivals(row_owner, row_sub, axes, loop_count, capacity)
    global_block = jnp.arange(slots, dtype=jnp.int32) // capacity * local_blocks + held_block
    block_count = cand.shape[1]
    block_onehot = (
        global_block[:, None] == jnp.arange(block_count, dtype=jnp.int32)[None, :]
    ).astype(jnp.bfloat16)
    cand_rows = jnp.dot(block_onehot, cand.astype(jnp.bfloat16), preferred_element_type=jnp.float32)
    near = (
        lax.dot_general(
            cand_rows.astype(jnp.bfloat16),
            block_onehot,
            (((1,), (1,)), ((), ())),
            preferred_element_type=jnp.float32,
        )
        > 0.5
    )
    averaged = attend(held_emb, near, sub)
    returned = lax.all_to_all(averaged, axes, split_axis=0, concat_axis=0, tiled=True)
    result = lax.dot_general(
        placing, returned, (((0,), (0,)), ((), ())), preferred_element_type=jnp.float32
    )
    return result.astype(jnp.bfloat16)


def solution(mesh):
    return jax.shard_map(
        body,
        mesh=mesh,
        in_specs=(
            P(("groups", "owner", "loop"), None),
            P(("groups", "owner", "loop")),
            P(("groups", "owner", "loop")),
            P("groups", None),
        ),
        out_specs=P(("groups", "owner", "loop"), None),
        check_vma=False,
    )
```

```python
import jax
import jax.numpy as jnp
from jax import lax
from jax.sharding import PartitionSpec as P

BLOCK = 128
SUB = 16
LABEL_COLUMNS = 128


def route(row_owner, row_sub, loop_count, capacity):
    devices = lax.axis_size("owner") * loop_count
    dest = row_owner * loop_count + row_sub % loop_count
    onehot = (dest[:, None] == jnp.arange(devices, dtype=jnp.int32)[None, :]).astype(jnp.bfloat16)
    rows = row_owner.shape[0]
    lower = (
        jnp.arange(rows, dtype=jnp.int32)[:, None] > jnp.arange(rows, dtype=jnp.int32)[None, :]
    ).astype(jnp.bfloat16)
    earlier = jnp.dot(lower, onehot, preferred_element_type=jnp.float32)
    within = jnp.sum(earlier * onehot.astype(jnp.float32), axis=1).astype(jnp.int32)
    return dest * capacity + within


def attend(keys, near, sub):
    slots = keys.shape[0]
    scale = 4.0 / keys.shape[1]
    scores = scale * lax.dot_general(
        keys, keys, (((1,), (1,)), ((), ())), preferred_element_type=jnp.float32
    )
    index = jnp.arange(slots, dtype=jnp.int32)
    same = (index[:, None] == index[None, :]) | (
        (sub[:, None] == sub[None, :]) & near
    )
    top = jnp.max(jnp.where(same, scores, jnp.float32(-1e30)), axis=1)
    weights = jnp.where(same, jnp.exp(scores - top[:, None]), jnp.float32(0.0))
    total = jnp.sum(weights, axis=1)
    summed = jnp.dot(weights.astype(jnp.bfloat16), keys, preferred_element_type=jnp.float32)
    return (summed / total[:, None]).astype(jnp.bfloat16)


def body(emb, row_owner, row_sub, cand):
    rows = emb.shape[0]
    owner_count = lax.axis_size("owner")
    loop_count = lax.axis_size("loop")
    devices = owner_count * loop_count
    capacity = 2 * rows // owner_count // loop_count
    slots = devices * capacity
    local_blocks = rows // BLOCK
    axes = ("owner", "loop")

    slot_of_row = route(row_owner, row_sub, loop_count, capacity)
    placing = (jnp.arange(slots, dtype=jnp.int32)[:, None] == slot_of_row[None, :]).astype(
        jnp.bfloat16
    )
    width = emb.shape[1]
    row_labels = jnp.stack(
        [jnp.arange(rows, dtype=jnp.int32) // BLOCK + 1, row_sub + 1], axis=1
    ).astype(jnp.bfloat16)
    labelled = jnp.concatenate(
        [emb, jnp.pad(row_labels, ((0, 0), (0, LABEL_COLUMNS - 2)))], axis=1
    )
    send = jnp.dot(placing, labelled, preferred_element_type=jnp.float32).astype(jnp.bfloat16)
    held = lax.all_to_all(send, axes, split_axis=0, concat_axis=0, tiled=True)
    held_emb = held[:, :width]
    held_labels = held[:, width : width + 2].astype(jnp.int32)

    index = jnp.arange(slots, dtype=jnp.int32)
    present = held_labels[:, 0] > 0
    source = index // capacity
    global_block = source * local_blocks + held_labels[:, 0] - 1
    global_block = jnp.where(present, global_block, 0)
    sub = jnp.where(present, held_labels[:, 1] - 1, -1 - index)
    block_count = cand.shape[1]
    block_onehot = (
        global_block[:, None] == jnp.arange(block_count, dtype=jnp.int32)[None, :]
    ).astype(jnp.bfloat16)
    cand_rows = jnp.dot(block_onehot, cand.astype(jnp.bfloat16), preferred_element_type=jnp.float32)
    near = (
        lax.dot_general(
            cand_rows.astype(jnp.bfloat16),
            block_onehot,
            (((1,), (1,)), ((), ())),
            preferred_element_type=jnp.float32,
        )
        > 0.5
    )
    averaged = attend(held_emb, near, sub)
    returned = lax.all_to_all(averaged, axes, split_axis=0, concat_axis=0, tiled=True)
    result = lax.dot_general(
        placing, returned, (((0,), (0,)), ((), ())), preferred_element_type=jnp.float32
    )
    return result.astype(jnp.bfloat16)


def solution(mesh):
    return jax.shard_map(
        body,
        mesh=mesh,
        in_specs=(
            P(("groups", "owner", "loop"), None),
            P(("groups", "owner", "loop")),
            P(("groups", "owner", "loop")),
            P("groups", None),
        ),
        out_specs=P(("groups", "owner", "loop"), None),
        check_vma=False,
    )
```

```python
import jax
import jax.numpy as jnp
from jax import lax
from jax.sharding import PartitionSpec as P

BLOCK = 128
SUB = 16
LABEL_COLUMNS = 128


def route(row_owner, row_sub, loop_count, capacity):
    devices = lax.axis_size("owner") * loop_count
    dest = row_owner * loop_count + row_sub % loop_count
    onehot = (dest[:, None] == jnp.arange(devices, dtype=jnp.int32)[None, :]).astype(jnp.bfloat16)
    rows = row_owner.shape[0]
    lower = (
        jnp.arange(rows, dtype=jnp.int32)[:, None] > jnp.arange(rows, dtype=jnp.int32)[None, :]
    ).astype(jnp.bfloat16)
    earlier = jnp.dot(lower, onehot, preferred_element_type=jnp.float32)
    within = jnp.sum(earlier * onehot.astype(jnp.float32), axis=1).astype(jnp.int32)
    return dest * capacity + within


def attend(keys, near, sub):
    slots = keys.shape[0]
    scale = 4.0 / keys.shape[1]
    scores = scale * lax.dot_general(
        keys, keys, (((1,), (1,)), ((), ())), preferred_element_type=jnp.float32
    )
    index = jnp.arange(slots, dtype=jnp.int32)
    same = (index[:, None] == index[None, :]) | (
        (sub[:, None] == sub[None, :]) & near
    )
    top = jnp.max(jnp.where(same, scores, jnp.float32(-1e30)), axis=1)
    weights = jnp.where(same, jnp.exp(scores - top[:, None]), jnp.float32(0.0))
    total = jnp.sum(weights, axis=1)
    summed = jnp.dot(weights.astype(jnp.bfloat16), keys, preferred_element_type=jnp.float32)
    return (summed / total[:, None]).astype(jnp.bfloat16)


def body(emb, row_owner, row_sub, cand):
    rows = emb.shape[0]
    owner_count = lax.axis_size("owner")
    loop_count = lax.axis_size("loop")
    devices = owner_count * loop_count
    capacity = 2 * rows // owner_count // loop_count
    slots = devices * capacity
    local_blocks = rows // BLOCK
    axes = ("owner", "loop")

    slot_of_row = route(row_owner, row_sub, loop_count, capacity)
    hit = jnp.arange(slots, dtype=jnp.int32)[:, None] == slot_of_row[None, :]
    source_row = jnp.sum(jnp.where(hit, jnp.arange(rows, dtype=jnp.int32)[None, :] - rows, 0), axis=1)
    source_row = source_row + rows
    width = emb.shape[1]
    row_labels = jnp.stack(
        [jnp.arange(rows, dtype=jnp.int32) // BLOCK + 1, row_sub + 1], axis=1
    ).astype(jnp.bfloat16)
    labelled = jnp.concatenate(
        [emb, jnp.pad(row_labels, ((0, 0), (0, LABEL_COLUMNS - 2)))], axis=1
    )
    send = jnp.take(labelled, source_row, axis=0, mode="fill", fill_value=0)
    held = lax.all_to_all(send, axes, split_axis=0, concat_axis=0, tiled=True)
    held_emb = held[:, :width]
    held_labels = held[:, width : width + 2].astype(jnp.int32)

    index = jnp.arange(slots, dtype=jnp.int32)
    present = held_labels[:, 0] > 0
    source = index // capacity
    global_block = source * local_blocks + held_labels[:, 0] - 1
    global_block = jnp.where(present, global_block, 0)
    sub = jnp.where(present, held_labels[:, 1] - 1, -1 - index)
    block_count = cand.shape[1]
    block_onehot = (
        global_block[:, None] == jnp.arange(block_count, dtype=jnp.int32)[None, :]
    ).astype(jnp.bfloat16)
    cand_rows = jnp.dot(block_onehot, cand.astype(jnp.bfloat16), preferred_element_type=jnp.float32)
    near = (
        lax.dot_general(
            cand_rows.astype(jnp.bfloat16),
            block_onehot,
            (((1,), (1,)), ((), ())),
            preferred_element_type=jnp.float32,
        )
        > 0.5
    )
    averaged = attend(held_emb, near, sub)
    returned = lax.all_to_all(averaged, axes, split_axis=0, concat_axis=0, tiled=True)
    return jnp.take(returned, slot_of_row, axis=0, mode="clip")


def solution(mesh):
    return jax.shard_map(
        body,
        mesh=mesh,
        in_specs=(
            P(("groups", "owner", "loop"), None),
            P(("groups", "owner", "loop")),
            P(("groups", "owner", "loop")),
            P("groups", None),
        ),
        out_specs=P(("groups", "owner", "loop"), None),
        check_vma=False,
    )
```

```python
import jax
import jax.numpy as jnp
from jax import lax
from jax.sharding import PartitionSpec as P

BLOCK = 128
SUB = 16
LABEL_COLUMNS = 128


PERMUTE_LIMIT = 16


def exchange(chunks, axes, devices, sign):
    if devices > PERMUTE_LIMIT:
        return lax.all_to_all(chunks, axes, split_axis=0, concat_axis=0, tiled=True)
    received = [chunks[0]]
    for k in range(1, devices):
        pairs = [(d, (d + sign * k) % devices) for d in range(devices)]
        received.append(lax.ppermute(chunks[k], axes, pairs))
    return jnp.stack(received)


def route(row_owner, row_sub, loop_count, capacity, me):
    devices = lax.axis_size("owner") * loop_count
    dest = (row_owner * loop_count + row_sub % loop_count - me) % devices
    onehot = (dest[:, None] == jnp.arange(devices, dtype=jnp.int32)[None, :]).astype(jnp.bfloat16)
    rows = row_owner.shape[0]
    lower = (
        jnp.arange(rows, dtype=jnp.int32)[:, None] > jnp.arange(rows, dtype=jnp.int32)[None, :]
    ).astype(jnp.bfloat16)
    earlier = jnp.dot(lower, onehot, preferred_element_type=jnp.float32)
    within = jnp.sum(earlier * onehot.astype(jnp.float32), axis=1).astype(jnp.int32)
    return dest * capacity + within


def attend(keys, near, sub):
    slots = keys.shape[0]
    scale = 4.0 / keys.shape[1]
    scores = scale * lax.dot_general(
        keys, keys, (((1,), (1,)), ((), ())), preferred_element_type=jnp.float32
    )
    index = jnp.arange(slots, dtype=jnp.int32)
    same = (index[:, None] == index[None, :]) | (
        (sub[:, None] == sub[None, :]) & near
    )
    top = jnp.max(jnp.where(same, scores, jnp.float32(-1e30)), axis=1)
    weights = jnp.where(same, jnp.exp(scores - top[:, None]), jnp.float32(0.0))
    total = jnp.sum(weights, axis=1)
    summed = jnp.dot(weights.astype(jnp.bfloat16), keys, preferred_element_type=jnp.float32)
    return (summed / total[:, None]).astype(jnp.bfloat16)


def body(emb, row_owner, row_sub, cand):
    rows = emb.shape[0]
    owner_count = lax.axis_size("owner")
    loop_count = lax.axis_size("loop")
    devices = owner_count * loop_count
    capacity = 2 * rows // owner_count // loop_count
    slots = devices * capacity
    local_blocks = rows // BLOCK
    axes = ("owner", "loop")

    me = lax.axis_index("owner") * loop_count + lax.axis_index("loop")
    if devices > PERMUTE_LIMIT:
        me = 0
    slot_of_row = route(row_owner, row_sub, loop_count, capacity, me)
    placing = (jnp.arange(slots, dtype=jnp.int32)[:, None] == slot_of_row[None, :]).astype(
        jnp.bfloat16
    )
    width = emb.shape[1]
    row_labels = jnp.stack(
        [jnp.arange(rows, dtype=jnp.int32) // BLOCK + 1, row_sub + 1], axis=1
    ).astype(jnp.bfloat16)
    labelled = jnp.concatenate(
        [emb, jnp.pad(row_labels, ((0, 0), (0, LABEL_COLUMNS - 2)))], axis=1
    )
    send = jnp.dot(placing, labelled, preferred_element_type=jnp.float32).astype(jnp.bfloat16)
    held = exchange(send.reshape(devices, capacity, send.shape[1]), axes, devices, 1)
    held = held.reshape(slots, send.shape[1])
    held_emb = held[:, :width]
    held_labels = held[:, width : width + 2].astype(jnp.int32)

    index = jnp.arange(slots, dtype=jnp.int32)
    present = held_labels[:, 0] > 0
    source = index // capacity
    if devices <= PERMUTE_LIMIT:
        source = (me - source) % devices
    global_block = source * local_blocks + held_labels[:, 0] - 1
    global_block = jnp.where(present, global_block, 0)
    sub = jnp.where(present, held_labels[:, 1] - 1, -1 - index)
    block_count = cand.shape[1]
    block_onehot = (
        global_block[:, None] == jnp.arange(block_count, dtype=jnp.int32)[None, :]
    ).astype(jnp.bfloat16)
    cand_rows = jnp.dot(block_onehot, cand.astype(jnp.bfloat16), preferred_element_type=jnp.float32)
    near = (
        lax.dot_general(
            cand_rows.astype(jnp.bfloat16),
            block_onehot,
            (((1,), (1,)), ((), ())),
            preferred_element_type=jnp.float32,
        )
        > 0.5
    )
    averaged = attend(held_emb, near, sub)
    returned = exchange(averaged.reshape(devices, capacity, width), axes, devices, -1)
    returned = returned.reshape(slots, width)
    result = lax.dot_general(
        placing, returned, (((0,), (0,)), ((), ())), preferred_element_type=jnp.float32
    )
    return result.astype(jnp.bfloat16)


def solution(mesh):
    return jax.shard_map(
        body,
        mesh=mesh,
        in_specs=(
            P(("groups", "owner", "loop"), None),
            P(("groups", "owner", "loop")),
            P(("groups", "owner", "loop")),
            P("groups", None),
        ),
        out_specs=P(("groups", "owner", "loop"), None),
        check_vma=False,
    )
```

```python
import functools

import jax
import jax.numpy as jnp
from jax import lax
from jax.experimental import pallas as pl
from jax.experimental.pallas import tpu as pltpu
from jax.sharding import PartitionSpec as P

BLOCK = 128
SUB = 16
LABEL_COLUMNS = 128


def route(row_owner, row_sub, loop_count, capacity):
    devices = lax.axis_size("owner") * loop_count
    dest = row_owner * loop_count + row_sub % loop_count
    onehot = (dest[:, None] == jnp.arange(devices, dtype=jnp.int32)[None, :]).astype(jnp.bfloat16)
    rows = row_owner.shape[0]
    lower = (
        jnp.arange(rows, dtype=jnp.int32)[:, None] > jnp.arange(rows, dtype=jnp.int32)[None, :]
    ).astype(jnp.bfloat16)
    earlier = jnp.dot(lower, onehot, preferred_element_type=jnp.float32)
    within = jnp.sum(earlier * onehot.astype(jnp.float32), axis=1).astype(jnp.int32)
    return dest * capacity + within


def attend_kernel(held_ref, cand_ref, base_col_ref, base_row_ref, out_ref, *, width):
    slots = held_ref.shape[0]
    block_count = cand_ref.shape[0]
    keys = held_ref[:, :width]
    labels = held_ref[:, width:].astype(jnp.float32)
    labels_t = labels.T
    index_col = lax.broadcasted_iota(jnp.int32, (slots, 1), 0)
    index_row = lax.broadcasted_iota(jnp.int32, (1, slots), 1)
    block_col = labels[:, 0:1].astype(jnp.int32)
    block_row = labels_t[0:1, :].astype(jnp.int32)
    sub_col = jnp.where(block_col > 0, labels[:, 1:2].astype(jnp.int32) - 1, -1 - index_col)
    sub_row = jnp.where(block_row > 0, labels_t[1:2, :].astype(jnp.int32) - 1, -1 - index_row)
    global_col = jnp.where(block_col > 0, base_col_ref[...] + block_col - 1, 0)
    global_row = jnp.where(block_row > 0, base_row_ref[...] + block_row - 1, 0)
    onehot = (global_col == lax.broadcasted_iota(jnp.int32, (1, block_count), 1)).astype(jnp.bfloat16)
    onehot_t = (lax.broadcasted_iota(jnp.int32, (block_count, 1), 0) == global_row).astype(
        jnp.bfloat16
    )
    cand_rows = jnp.dot(onehot, cand_ref[...], preferred_element_type=jnp.float32)
    near = jnp.dot(cand_rows.astype(jnp.bfloat16), onehot_t, preferred_element_type=jnp.float32) > 0.5
    scale = 4.0 / width
    scores = scale * lax.dot_general(
        keys, keys, (((1,), (1,)), ((), ())), preferred_element_type=jnp.float32
    )
    same = (index_col == index_row) | ((sub_col == sub_row) & near)
    top = jnp.max(jnp.where(same, scores, jnp.float32(-1e30)), axis=1, keepdims=True)
    weights = jnp.where(same, jnp.exp(scores - top), jnp.float32(0.0))
    total = jnp.sum(weights, axis=1, keepdims=True)
    summed = jnp.dot(weights.astype(jnp.bfloat16), keys, preferred_element_type=jnp.float32)
    out_ref[...] = (summed / total).astype(out_ref.dtype)


def attend(held, cand, capacity, local_blocks, width):
    slots = held.shape[0]
    base = jnp.arange(slots, dtype=jnp.int32) // capacity * local_blocks
    vmem = pl.BlockSpec(memory_space=pltpu.VMEM)
    cost = pl.CostEstimate(
        flops=4 * slots * slots * width,
        transcendentals=slots * slots,
        bytes_accessed=held.size * 2 + slots * width * 2,
    )
    return pl.pallas_call(
        functools.partial(attend_kernel, width=width),
        out_shape=jax.ShapeDtypeStruct((slots, width), jnp.bfloat16),
        in_specs=[vmem] * 4,
        out_specs=vmem,
        cost_estimate=cost,
    )(held, cand.astype(jnp.bfloat16), base[:, None], base[None, :])


def body(emb, row_owner, row_sub, cand):
    rows = emb.shape[0]
    owner_count = lax.axis_size("owner")
    loop_count = lax.axis_size("loop")
    devices = owner_count * loop_count
    capacity = 2 * rows // owner_count // loop_count
    slots = devices * capacity
    local_blocks = rows // BLOCK
    axes = ("owner", "loop")

    slot_of_row = route(row_owner, row_sub, loop_count, capacity)
    placing = (jnp.arange(slots, dtype=jnp.int32)[:, None] == slot_of_row[None, :]).astype(
        jnp.bfloat16
    )
    width = emb.shape[1]
    row_labels = jnp.stack(
        [jnp.arange(rows, dtype=jnp.int32) // BLOCK + 1, row_sub + 1], axis=1
    ).astype(jnp.bfloat16)
    labelled = jnp.concatenate(
        [emb, jnp.pad(row_labels, ((0, 0), (0, LABEL_COLUMNS - 2)))], axis=1
    )
    send = jnp.dot(placing, labelled, preferred_element_type=jnp.float32).astype(jnp.bfloat16)
    held = lax.all_to_all(send, axes, split_axis=0, concat_axis=0, tiled=True)
    averaged = attend(held, cand, capacity, local_blocks, width)
    returned = lax.all_to_all(averaged, axes, split_axis=0, concat_axis=0, tiled=True)
    result = lax.dot_general(
        placing, returned, (((0,), (0,)), ((), ())), preferred_element_type=jnp.float32
    )
    return result.astype(jnp.bfloat16)


def solution(mesh):
    return jax.shard_map(
        body,
        mesh=mesh,
        in_specs=(
            P(("groups", "owner", "loop"), None),
            P(("groups", "owner", "loop")),
            P(("groups", "owner", "loop")),
            P("groups", None),
        ),
        out_specs=P(("groups", "owner", "loop"), None),
        check_vma=False,
    )
```

```python
import functools

import jax
import jax.numpy as jnp
from jax import lax
from jax.experimental import pallas as pl
from jax.experimental.pallas import tpu as pltpu
from jax.sharding import PartitionSpec as P

BLOCK = 128
SUB = 16
LABEL_COLUMNS = 128


def place_kernel(emb_ref, owner_ref, sub_ref, send_ref, slot_ref, *, loop_count, capacity, devices):
    rows, width = emb_ref.shape
    slots = send_ref.shape[0]
    owner = owner_ref[...]
    sub = sub_ref[...]
    dest = owner * loop_count + sub % loop_count
    onehot_t = (lax.broadcasted_iota(jnp.int32, (devices, rows), 0) == dest).astype(jnp.bfloat16)
    upper = (
        lax.broadcasted_iota(jnp.int32, (rows, rows), 0)
        < lax.broadcasted_iota(jnp.int32, (rows, rows), 1)
    ).astype(jnp.bfloat16)
    earlier_t = jnp.dot(onehot_t, upper, preferred_element_type=jnp.float32)
    within = jnp.sum(earlier_t * onehot_t.astype(jnp.float32), axis=0, keepdims=True)
    slot = dest * capacity + within.astype(jnp.int32)
    slot_ref[...] = slot
    placing = (lax.broadcasted_iota(jnp.int32, (slots, rows), 0) == slot).astype(jnp.bfloat16)
    send_ref[:, :width] = jnp.dot(
        placing, emb_ref[...], preferred_element_type=jnp.float32
    ).astype(send_ref.dtype)
    which = lax.broadcasted_iota(jnp.int32, (LABEL_COLUMNS, rows), 0)
    block = lax.broadcasted_iota(jnp.int32, (LABEL_COLUMNS, rows), 1) // BLOCK
    labels_t = jnp.where(which == 0, block + 1, jnp.where(which == 1, sub + 1, 0))
    labels = labels_t.astype(jnp.float32).T.astype(jnp.bfloat16)
    send_ref[:, width:] = jnp.dot(
        placing, labels, preferred_element_type=jnp.float32
    ).astype(send_ref.dtype)


def place(emb, row_owner, row_sub, loop_count, capacity, devices):
    rows, width = emb.shape
    slots = devices * capacity
    vmem = pl.BlockSpec(memory_space=pltpu.VMEM)
    cost = pl.CostEstimate(
        flops=2 * slots * rows * (width + LABEL_COLUMNS) + 2 * devices * rows * rows,
        transcendentals=0,
        bytes_accessed=rows * width * 2 + slots * (width + LABEL_COLUMNS) * 2,
    )
    return pl.pallas_call(
        functools.partial(
            place_kernel, loop_count=loop_count, capacity=capacity, devices=devices
        ),
        out_shape=(
            jax.ShapeDtypeStruct((slots, width + LABEL_COLUMNS), jnp.bfloat16),
            jax.ShapeDtypeStruct((1, rows), jnp.int32),
        ),
        in_specs=[vmem] * 3,
        out_specs=(vmem, vmem),
        cost_estimate=cost,
    )(emb, row_owner[None, :], row_sub[None, :])


def attend(keys, near, sub):
    slots = keys.shape[0]
    scale = 4.0 / keys.shape[1]
    scores = scale * lax.dot_general(
        keys, keys, (((1,), (1,)), ((), ())), preferred_element_type=jnp.float32
    )
    index = jnp.arange(slots, dtype=jnp.int32)
    same = (index[:, None] == index[None, :]) | (
        (sub[:, None] == sub[None, :]) & near
    )
    top = jnp.max(jnp.where(same, scores, jnp.float32(-1e30)), axis=1)
    weights = jnp.where(same, jnp.exp(scores - top[:, None]), jnp.float32(0.0))
    total = jnp.sum(weights, axis=1)
    summed = jnp.dot(weights.astype(jnp.bfloat16), keys, preferred_element_type=jnp.float32)
    return (summed / total[:, None]).astype(jnp.bfloat16)


def body(emb, row_owner, row_sub, cand):
    rows = emb.shape[0]
    owner_count = lax.axis_size("owner")
    loop_count = lax.axis_size("loop")
    devices = owner_count * loop_count
    capacity = 2 * rows // owner_count // loop_count
    slots = devices * capacity
    local_blocks = rows // BLOCK
    axes = ("owner", "loop")

    send, slot_of_row = place(emb, row_owner, row_sub, loop_count, capacity, devices)
    slot_of_row = slot_of_row[0]
    placing = (jnp.arange(slots, dtype=jnp.int32)[:, None] == slot_of_row[None, :]).astype(
        jnp.bfloat16
    )
    width = emb.shape[1]
    held = lax.all_to_all(send, axes, split_axis=0, concat_axis=0, tiled=True)
    held_emb = held[:, :width]
    held_labels = held[:, width : width + 2].astype(jnp.int32)

    index = jnp.arange(slots, dtype=jnp.int32)
    present = held_labels[:, 0] > 0
    source = index // capacity
    global_block = source * local_blocks + held_labels[:, 0] - 1
    global_block = jnp.where(present, global_block, 0)
    sub = jnp.where(present, held_labels[:, 1] - 1, -1 - index)
    block_count = cand.shape[1]
    block_onehot = (
        global_block[:, None] == jnp.arange(block_count, dtype=jnp.int32)[None, :]
    ).astype(jnp.bfloat16)
    cand_rows = jnp.dot(block_onehot, cand.astype(jnp.bfloat16), preferred_element_type=jnp.float32)
    near = (
        lax.dot_general(
            cand_rows.astype(jnp.bfloat16),
            block_onehot,
            (((1,), (1,)), ((), ())),
            preferred_element_type=jnp.float32,
        )
        > 0.5
    )
    averaged = attend(held_emb, near, sub)
    returned = lax.all_to_all(averaged, axes, split_axis=0, concat_axis=0, tiled=True)
    result = lax.dot_general(
        placing, returned, (((0,), (0,)), ((), ())), preferred_element_type=jnp.float32
    )
    return result.astype(jnp.bfloat16)


def solution(mesh):
    return jax.shard_map(
        body,
        mesh=mesh,
        in_specs=(
            P(("groups", "owner", "loop"), None),
            P(("groups", "owner", "loop")),
            P(("groups", "owner", "loop")),
            P("groups", None),
        ),
        out_specs=P(("groups", "owner", "loop"), None),
        check_vma=False,
    )
```

```python
import functools

import jax
import jax.numpy as jnp
from jax import lax
from jax.experimental import pallas as pl
from jax.experimental.pallas import tpu as pltpu
from jax.sharding import PartitionSpec as P

BLOCK = 128
SUB = 16
LABEL_COLUMNS = 128
PLACE_STEP = 128


def place_kernel(
    emb_ref, owner_ref, sub_ref, send_ref, slot_ref, labels_ref, *, loop_count, capacity, devices
):
    rows, width = emb_ref.shape
    step_slots = send_ref.shape[0]
    step = pl.program_id(0)

    @pl.when(step == 0)
    def _():
        owner = owner_ref[...]
        sub = sub_ref[...]
        dest = owner * loop_count + sub % loop_count
        onehot_t = (lax.broadcasted_iota(jnp.int32, (devices, rows), 0) == dest).astype(
            jnp.bfloat16
        )
        upper = (
            lax.broadcasted_iota(jnp.int32, (rows, rows), 0)
            < lax.broadcasted_iota(jnp.int32, (rows, rows), 1)
        ).astype(jnp.bfloat16)
        earlier_t = jnp.dot(onehot_t, upper, preferred_element_type=jnp.float32)
        within = jnp.sum(earlier_t * onehot_t.astype(jnp.float32), axis=0, keepdims=True)
        slot_ref[...] = dest * capacity + within.astype(jnp.int32)
        which = lax.broadcasted_iota(jnp.int32, (LABEL_COLUMNS, rows), 0)
        block = lax.broadcasted_iota(jnp.int32, (LABEL_COLUMNS, rows), 1) // BLOCK
        labels_t = jnp.where(which == 0, block + 1, jnp.where(which == 1, sub + 1, 0))
        labels_ref[...] = labels_t.astype(jnp.float32).T.astype(jnp.bfloat16)

    first = step * step_slots
    placing = (
        lax.broadcasted_iota(jnp.int32, (step_slots, rows), 0) + first == slot_ref[...]
    ).astype(jnp.bfloat16)
    send_ref[:, :width] = jnp.dot(
        placing, emb_ref[...], preferred_element_type=jnp.float32
    ).astype(send_ref.dtype)
    send_ref[:, width:] = jnp.dot(
        placing, labels_ref[...], preferred_element_type=jnp.float32
    ).astype(send_ref.dtype)


def place(emb, row_owner, row_sub, loop_count, capacity, devices):
    rows, width = emb.shape
    slots = devices * capacity
    step_slots = min(slots, PLACE_STEP)
    cost = pl.CostEstimate(
        flops=2 * slots * rows * (width + LABEL_COLUMNS) + 2 * devices * rows * rows,
        transcendentals=0,
        bytes_accessed=rows * width * 2 + slots * (width + LABEL_COLUMNS) * 2,
    )
    whole = lambda step: (0, 0)
    return pl.pallas_call(
        functools.partial(
            place_kernel, loop_count=loop_count, capacity=capacity, devices=devices
        ),
        grid=(slots // step_slots,),
        out_shape=(
            jax.ShapeDtypeStruct((slots, width + LABEL_COLUMNS), jnp.bfloat16),
            jax.ShapeDtypeStruct((1, rows), jnp.int32),
        ),
        in_specs=[
            pl.BlockSpec((rows, width), whole),
            pl.BlockSpec((1, rows), whole),
            pl.BlockSpec((1, rows), whole),
        ],
        out_specs=(
            pl.BlockSpec((step_slots, width + LABEL_COLUMNS), lambda step: (step, 0)),
            pl.BlockSpec((1, rows), whole),
        ),
        scratch_shapes=[pltpu.VMEM((rows, LABEL_COLUMNS), jnp.bfloat16)],
        compiler_params=pltpu.CompilerParams(dimension_semantics=("arbitrary",)),
        cost_estimate=cost,
    )(emb, row_owner[None, :], row_sub[None, :])


def attend(keys, near, sub):
    slots = keys.shape[0]
    scale = 4.0 / keys.shape[1]
    scores = scale * lax.dot_general(
        keys, keys, (((1,), (1,)), ((), ())), preferred_element_type=jnp.float32
    )
    index = jnp.arange(slots, dtype=jnp.int32)
    same = (index[:, None] == index[None, :]) | (
        (sub[:, None] == sub[None, :]) & near
    )
    top = jnp.max(jnp.where(same, scores, jnp.float32(-1e30)), axis=1)
    weights = jnp.where(same, jnp.exp(scores - top[:, None]), jnp.float32(0.0))
    total = jnp.sum(weights, axis=1)
    summed = jnp.dot(weights.astype(jnp.bfloat16), keys, preferred_element_type=jnp.float32)
    return (summed / total[:, None]).astype(jnp.bfloat16)


def body(emb, row_owner, row_sub, cand):
    rows = emb.shape[0]
    owner_count = lax.axis_size("owner")
    loop_count = lax.axis_size("loop")
    devices = owner_count * loop_count
    capacity = 2 * rows // owner_count // loop_count
    slots = devices * capacity
    local_blocks = rows // BLOCK
    axes = ("owner", "loop")

    send, slot_of_row = place(emb, row_owner, row_sub, loop_count, capacity, devices)
    slot_of_row = slot_of_row[0]
    placing = (jnp.arange(slots, dtype=jnp.int32)[:, None] == slot_of_row[None, :]).astype(
        jnp.bfloat16
    )
    width = emb.shape[1]
    held = lax.all_to_all(send, axes, split_axis=0, concat_axis=0, tiled=True)
    held_emb = held[:, :width]
    held_labels = held[:, width : width + 2].astype(jnp.int32)

    index = jnp.arange(slots, dtype=jnp.int32)
    present = held_labels[:, 0] > 0
    source = index // capacity
    global_block = source * local_blocks + held_labels[:, 0] - 1
    global_block = jnp.where(present, global_block, 0)
    sub = jnp.where(present, held_labels[:, 1] - 1, -1 - index)
    block_count = cand.shape[1]
    block_onehot = (
        global_block[:, None] == jnp.arange(block_count, dtype=jnp.int32)[None, :]
    ).astype(jnp.bfloat16)
    cand_rows = jnp.dot(block_onehot, cand.astype(jnp.bfloat16), preferred_element_type=jnp.float32)
    near = (
        lax.dot_general(
            cand_rows.astype(jnp.bfloat16),
            block_onehot,
            (((1,), (1,)), ((), ())),
            preferred_element_type=jnp.float32,
        )
        > 0.5
    )
    averaged = attend(held_emb, near, sub)
    returned = lax.all_to_all(averaged, axes, split_axis=0, concat_axis=0, tiled=True)
    result = lax.dot_general(
        placing, returned, (((0,), (0,)), ((), ())), preferred_element_type=jnp.float32
    )
    return result.astype(jnp.bfloat16)


def solution(mesh):
    return jax.shard_map(
        body,
        mesh=mesh,
        in_specs=(
            P(("groups", "owner", "loop"), None),
            P(("groups", "owner", "loop")),
            P(("groups", "owner", "loop")),
            P("groups", None),
        ),
        out_specs=P(("groups", "owner", "loop"), None),
        check_vma=False,
    )
```

```python
import functools

import jax
import jax.numpy as jnp
from jax import lax
from jax.experimental import pallas as pl
from jax.experimental.pallas import tpu as pltpu
from jax.sharding import PartitionSpec as P

BLOCK = 128
SUB = 16
LABEL_COLUMNS = 128
TILE = 16


def place_kernel(
    emb_ref, owner_ref, sub_ref, send_ref, slot_ref, *, loop_count, capacity, devices, tiled
):
    rows, width = emb_ref.shape
    slots = devices * capacity
    owner = owner_ref[...]
    sub = sub_ref[...]
    dest = owner * loop_count + sub % loop_count
    onehot_t = (lax.broadcasted_iota(jnp.int32, (devices, rows), 0) == dest).astype(jnp.bfloat16)
    upper = (
        lax.broadcasted_iota(jnp.int32, (rows, rows), 0)
        < lax.broadcasted_iota(jnp.int32, (rows, rows), 1)
    ).astype(jnp.bfloat16)
    earlier_t = jnp.dot(onehot_t, upper, preferred_element_type=jnp.float32)
    within = jnp.sum(earlier_t * onehot_t.astype(jnp.float32), axis=0, keepdims=True)
    slot = dest * capacity + within.astype(jnp.int32)
    slot_ref[...] = slot
    placing = (lax.broadcasted_iota(jnp.int32, (slots, rows), 0) == slot).astype(jnp.bfloat16)
    placed = jnp.dot(placing, emb_ref[...], preferred_element_type=jnp.float32).astype(
        send_ref.dtype
    )
    which = lax.broadcasted_iota(jnp.int32, (LABEL_COLUMNS, rows), 0)
    block = lax.broadcasted_iota(jnp.int32, (LABEL_COLUMNS, rows), 1) // BLOCK
    column = 0
    if tiled:
        column = slot % capacity // TILE * 2
    labels_t = jnp.where(which == column, block + 1, jnp.where(which == column + 1, sub + 1, 0))
    labels = labels_t.astype(jnp.float32).T.astype(jnp.bfloat16)
    placed_labels = jnp.dot(placing, labels, preferred_element_type=jnp.float32).astype(
        send_ref.dtype
    )
    if not tiled:
        send_ref[:, :width] = placed
        send_ref[:, width:] = placed_labels
        return
    row_tiles = capacity // TILE
    col_tiles = width // LABEL_COLUMNS
    for chunk in range(devices):
        base = chunk * capacity
        for a in range(row_tiles):
            for e in range(col_tiles):
                send_ref[chunk, (a * col_tiles + e) * TILE : (a * col_tiles + e + 1) * TILE, :] = placed[
                    base + a * TILE : base + (a + 1) * TILE, e * LABEL_COLUMNS : (e + 1) * LABEL_COLUMNS
                ]
        tile = placed_labels[base : base + TILE]
        for a in range(1, row_tiles):
            tile = tile + placed_labels[base + a * TILE : base + (a + 1) * TILE]
        send_ref[chunk, row_tiles * col_tiles * TILE :, :] = tile


def place(emb, row_owner, row_sub, loop_count, capacity, devices, tiled):
    rows, width = emb.shape
    slots = devices * capacity
    vmem = pl.BlockSpec(memory_space=pltpu.VMEM)
    cost = pl.CostEstimate(
        flops=2 * slots * rows * (width + LABEL_COLUMNS) + 2 * devices * rows * rows,
        transcendentals=0,
        bytes_accessed=rows * width * 2 + slots * (width + LABEL_COLUMNS) * 2,
    )
    if tiled:
        shape = (devices, capacity * width // LABEL_COLUMNS + TILE, LABEL_COLUMNS)
    else:
        shape = (slots, width + LABEL_COLUMNS)
    return pl.pallas_call(
        functools.partial(
            place_kernel, loop_count=loop_count, capacity=capacity, devices=devices, tiled=tiled
        ),
        out_shape=(
            jax.ShapeDtypeStruct(shape, jnp.bfloat16),
            jax.ShapeDtypeStruct((1, rows), jnp.int32),
        ),
        in_specs=[vmem] * 3,
        out_specs=(vmem, vmem),
        cost_estimate=cost,
    )(emb, row_owner[None, :], row_sub[None, :])


def attend(keys, near, sub):
    slots = keys.shape[0]
    scale = 4.0 / keys.shape[1]
    scores = scale * lax.dot_general(
        keys, keys, (((1,), (1,)), ((), ())), preferred_element_type=jnp.float32
    )
    index = jnp.arange(slots, dtype=jnp.int32)
    same = (index[:, None] == index[None, :]) | (
        (sub[:, None] == sub[None, :]) & near
    )
    top = jnp.max(jnp.where(same, scores, jnp.float32(-1e30)), axis=1)
    weights = jnp.where(same, jnp.exp(scores - top[:, None]), jnp.float32(0.0))
    total = jnp.sum(weights, axis=1)
    summed = jnp.dot(weights.astype(jnp.bfloat16), keys, preferred_element_type=jnp.float32)
    return (summed / total[:, None]).astype(jnp.bfloat16)


def body(emb, row_owner, row_sub, cand):
    rows = emb.shape[0]
    owner_count = lax.axis_size("owner")
    loop_count = lax.axis_size("loop")
    devices = owner_count * loop_count
    capacity = 2 * rows // owner_count // loop_count
    slots = devices * capacity
    local_blocks = rows // BLOCK
    axes = ("owner", "loop")

    width = emb.shape[1]
    tiled = capacity % TILE == 0 and width % LABEL_COLUMNS == 0
    send, slot_of_row = place(emb, row_owner, row_sub, loop_count, capacity, devices, tiled)
    slot_of_row = slot_of_row[0]
    placing = (jnp.arange(slots, dtype=jnp.int32)[:, None] == slot_of_row[None, :]).astype(
        jnp.bfloat16
    )
    held = lax.all_to_all(send, axes, split_axis=0, concat_axis=0, tiled=True)
    if tiled:
        row_tiles = capacity // TILE
        col_tiles = width // LABEL_COLUMNS
        body_rows = row_tiles * col_tiles * TILE
        held_emb = held[:, :body_rows].reshape(devices, row_tiles, col_tiles, TILE, LABEL_COLUMNS)
        held_emb = held_emb.transpose(0, 1, 3, 2, 4).reshape(slots, width)
        held_labels = held[:, body_rows:, : 2 * row_tiles].reshape(devices, TILE, row_tiles, 2)
        held_labels = held_labels.transpose(0, 2, 1, 3).reshape(slots, 2).astype(jnp.int32)
    else:
        held_emb = held[:, :width]
        held_labels = held[:, width : width + 2].astype(jnp.int32)

    index = jnp.arange(slots, dtype=jnp.int32)
    present = held_labels[:, 0] > 0
    source = index // capacity
    global_block = source * local_blocks + held_labels[:, 0] - 1
    global_block = jnp.where(present, global_block, 0)
    sub = jnp.where(present, held_labels[:, 1] - 1, -1 - index)
    block_count = cand.shape[1]
    block_onehot = (
        global_block[:, None] == jnp.arange(block_count, dtype=jnp.int32)[None, :]
    ).astype(jnp.bfloat16)
    cand_rows = jnp.dot(block_onehot, cand.astype(jnp.bfloat16), preferred_element_type=jnp.float32)
    near = (
        lax.dot_general(
            cand_rows.astype(jnp.bfloat16),
            block_onehot,
            (((1,), (1,)), ((), ())),
            preferred_element_type=jnp.float32,
        )
        > 0.5
    )
    averaged = attend(held_emb, near, sub)
    returned = lax.all_to_all(averaged, axes, split_axis=0, concat_axis=0, tiled=True)
    result = lax.dot_general(
        placing, returned, (((0,), (0,)), ((), ())), preferred_element_type=jnp.float32
    )
    return result.astype(jnp.bfloat16)


def solution(mesh):
    return jax.shard_map(
        body,
        mesh=mesh,
        in_specs=(
            P(("groups", "owner", "loop"), None),
            P(("groups", "owner", "loop")),
            P(("groups", "owner", "loop")),
            P("groups", None),
        ),
        out_specs=P(("groups", "owner", "loop"), None),
        check_vma=False,
    )
```

```python
import functools

import jax
import jax.numpy as jnp
from jax import lax
from jax.experimental import pallas as pl
from jax.experimental.pallas import tpu as pltpu
from jax.sharding import PartitionSpec as P

BLOCK = 128
SUB = 16
LABEL_COLUMNS = 128
TILE = 16
PLACE_GROUPS = 4


def place_tiled_kernel(
    emb_hbm, owner_ref, sub_ref, send_hbm, slot_ref, emb_vmem, stage, sems, *, loop_count, capacity, devices
):
    rows, width = emb_vmem.shape
    slots = devices * capacity
    groups = stage.shape[0]
    group_chunks = devices // groups
    load = pltpu.make_async_copy(emb_hbm, emb_vmem, sems.at[0])
    load.start()
    owner = owner_ref[...]
    sub = sub_ref[...]
    dest = owner * loop_count + sub % loop_count
    onehot_t = (lax.broadcasted_iota(jnp.int32, (devices, rows), 0) == dest).astype(jnp.bfloat16)
    upper = (
        lax.broadcasted_iota(jnp.int32, (rows, rows), 0)
        < lax.broadcasted_iota(jnp.int32, (rows, rows), 1)
    ).astype(jnp.bfloat16)
    earlier_t = jnp.dot(onehot_t, upper, preferred_element_type=jnp.float32)
    within = jnp.sum(earlier_t * onehot_t.astype(jnp.float32), axis=0, keepdims=True)
    slot = dest * capacity + within.astype(jnp.int32)
    slot_ref[...] = slot
    placing = (lax.broadcasted_iota(jnp.int32, (slots, rows), 0) == slot).astype(jnp.bfloat16)
    which = lax.broadcasted_iota(jnp.int32, (LABEL_COLUMNS, rows), 0)
    block = lax.broadcasted_iota(jnp.int32, (LABEL_COLUMNS, rows), 1) // BLOCK
    column = slot % capacity // TILE * 2
    labels_t = jnp.where(which == column, block + 1, jnp.where(which == column + 1, sub + 1, 0))
    labels = labels_t.astype(jnp.float32).T.astype(jnp.bfloat16)
    placed_labels = jnp.dot(placing, labels, preferred_element_type=jnp.float32).astype(
        stage.dtype
    )
    row_tiles = capacity // TILE
    col_tiles = width // LABEL_COLUMNS
    load.wait()
    stores = []
    for g in range(groups):
        first = g * group_chunks * capacity
        placed = jnp.dot(
            placing[first : first + group_chunks * capacity],
            emb_vmem[...],
            preferred_element_type=jnp.float32,
        ).astype(stage.dtype)
        for c in range(group_chunks):
            base = c * capacity
            for a in range(row_tiles):
                for e in range(col_tiles):
                    t = a * col_tiles + e
                    stage[g, c, t * TILE : (t + 1) * TILE, :] = placed[
                        base + a * TILE : base + (a + 1) * TILE,
                        e * LABEL_COLUMNS : (e + 1) * LABEL_COLUMNS,
                    ]
            tile = placed_labels[first + base : first + base + TILE]
            for a in range(1, row_tiles):
                tile = tile + placed_labels[first + base + a * TILE : first + base + (a + 1) * TILE]
            stage[g, c, row_tiles * col_tiles * TILE :, :] = tile
        store = pltpu.make_async_copy(
            stage.at[g], send_hbm.at[g * group_chunks : (g + 1) * group_chunks], sems.at[1 + g]
        )
        store.start()
        stores.append(store)
    for store in stores:
        store.wait()


def place_kernel(
    emb_ref, owner_ref, sub_ref, send_ref, slot_ref, *, loop_count, capacity, devices, tiled
):
    rows, width = emb_ref.shape
    slots = devices * capacity
    owner = owner_ref[...]
    sub = sub_ref[...]
    dest = owner * loop_count + sub % loop_count
    onehot_t = (lax.broadcasted_iota(jnp.int32, (devices, rows), 0) == dest).astype(jnp.bfloat16)
    upper = (
        lax.broadcasted_iota(jnp.int32, (rows, rows), 0)
        < lax.broadcasted_iota(jnp.int32, (rows, rows), 1)
    ).astype(jnp.bfloat16)
    earlier_t = jnp.dot(onehot_t, upper, preferred_element_type=jnp.float32)
    within = jnp.sum(earlier_t * onehot_t.astype(jnp.float32), axis=0, keepdims=True)
    slot = dest * capacity + within.astype(jnp.int32)
    slot_ref[...] = slot
    placing = (lax.broadcasted_iota(jnp.int32, (slots, rows), 0) == slot).astype(jnp.bfloat16)
    placed = jnp.dot(placing, emb_ref[...], preferred_element_type=jnp.float32).astype(
        send_ref.dtype
    )
    which = lax.broadcasted_iota(jnp.int32, (LABEL_COLUMNS, rows), 0)
    block = lax.broadcasted_iota(jnp.int32, (LABEL_COLUMNS, rows), 1) // BLOCK
    column = 0
    if tiled:
        column = slot % capacity // TILE * 2
    labels_t = jnp.where(which == column, block + 1, jnp.where(which == column + 1, sub + 1, 0))
    labels = labels_t.astype(jnp.float32).T.astype(jnp.bfloat16)
    placed_labels = jnp.dot(placing, labels, preferred_element_type=jnp.float32).astype(
        send_ref.dtype
    )
    if not tiled:
        send_ref[:, :width] = placed
        send_ref[:, width:] = placed_labels
        return
    row_tiles = capacity // TILE
    col_tiles = width // LABEL_COLUMNS
    for chunk in range(devices):
        base = chunk * capacity
        for a in range(row_tiles):
            for e in range(col_tiles):
                send_ref[chunk, (a * col_tiles + e) * TILE : (a * col_tiles + e + 1) * TILE, :] = placed[
                    base + a * TILE : base + (a + 1) * TILE, e * LABEL_COLUMNS : (e + 1) * LABEL_COLUMNS
                ]
        tile = placed_labels[base : base + TILE]
        for a in range(1, row_tiles):
            tile = tile + placed_labels[base + a * TILE : base + (a + 1) * TILE]
        send_ref[chunk, row_tiles * col_tiles * TILE :, :] = tile


def place(emb, row_owner, row_sub, loop_count, capacity, devices, tiled):
    rows, width = emb.shape
    slots = devices * capacity
    vmem = pl.BlockSpec(memory_space=pltpu.VMEM)
    cost = pl.CostEstimate(
        flops=2 * slots * rows * (width + LABEL_COLUMNS) + 2 * devices * rows * rows,
        transcendentals=0,
        bytes_accessed=rows * width * 2 + slots * (width + LABEL_COLUMNS) * 2,
    )
    if tiled:
        chunk_rows = capacity * width // LABEL_COLUMNS + TILE
        groups = PLACE_GROUPS if devices % PLACE_GROUPS == 0 else 1
        return pl.pallas_call(
            functools.partial(
                place_tiled_kernel, loop_count=loop_count, capacity=capacity, devices=devices
            ),
            out_shape=(
                jax.ShapeDtypeStruct((devices, chunk_rows, LABEL_COLUMNS), jnp.bfloat16),
                jax.ShapeDtypeStruct((1, rows), jnp.int32),
            ),
            in_specs=[pl.BlockSpec(memory_space=pl.ANY), vmem, vmem],
            out_specs=(pl.BlockSpec(memory_space=pl.ANY), vmem),
            scratch_shapes=[
                pltpu.VMEM((rows, width), jnp.bfloat16),
                pltpu.VMEM((groups, devices // groups, chunk_rows, LABEL_COLUMNS), jnp.bfloat16),
                pltpu.SemaphoreType.DMA((1 + groups,)),
            ],
            cost_estimate=cost,
        )(emb, row_owner[None, :], row_sub[None, :])
    shape = (slots, width + LABEL_COLUMNS)
    return pl.pallas_call(
        functools.partial(
            place_kernel, loop_count=loop_count, capacity=capacity, devices=devices, tiled=tiled
        ),
        out_shape=(
            jax.ShapeDtypeStruct(shape, jnp.bfloat16),
            jax.ShapeDtypeStruct((1, rows), jnp.int32),
        ),
        in_specs=[vmem] * 3,
        out_specs=(vmem, vmem),
        cost_estimate=cost,
    )(emb, row_owner[None, :], row_sub[None, :])


def attend(keys, near, sub):
    slots = keys.shape[0]
    scale = 4.0 / keys.shape[1]
    scores = scale * lax.dot_general(
        keys, keys, (((1,), (1,)), ((), ())), preferred_element_type=jnp.float32
    )
    index = jnp.arange(slots, dtype=jnp.int32)
    same = (index[:, None] == index[None, :]) | (
        (sub[:, None] == sub[None, :]) & near
    )
    top = jnp.max(jnp.where(same, scores, jnp.float32(-1e30)), axis=1)
    weights = jnp.where(same, jnp.exp(scores - top[:, None]), jnp.float32(0.0))
    total = jnp.sum(weights, axis=1)
    summed = jnp.dot(weights.astype(jnp.bfloat16), keys, preferred_element_type=jnp.float32)
    return (summed / total[:, None]).astype(jnp.bfloat16)


def body(emb, row_owner, row_sub, cand):
    rows = emb.shape[0]
    owner_count = lax.axis_size("owner")
    loop_count = lax.axis_size("loop")
    devices = owner_count * loop_count
    capacity = 2 * rows // owner_count // loop_count
    slots = devices * capacity
    local_blocks = rows // BLOCK
    axes = ("owner", "loop")

    width = emb.shape[1]
    tiled = capacity % TILE == 0 and width % LABEL_COLUMNS == 0
    send, slot_of_row = place(emb, row_owner, row_sub, loop_count, capacity, devices, tiled)
    slot_of_row = slot_of_row[0]
    placing = (jnp.arange(slots, dtype=jnp.int32)[:, None] == slot_of_row[None, :]).astype(
        jnp.bfloat16
    )
    held = lax.all_to_all(send, axes, split_axis=0, concat_axis=0, tiled=True)
    if tiled:
        row_tiles = capacity // TILE
        col_tiles = width // LABEL_COLUMNS
        body_rows = row_tiles * col_tiles * TILE
        held_emb = held[:, :body_rows].reshape(devices, row_tiles, col_tiles, TILE, LABEL_COLUMNS)
        held_emb = held_emb.transpose(0, 1, 3, 2, 4).reshape(slots, width)
        held_labels = held[:, body_rows:, : 2 * row_tiles].reshape(devices, TILE, row_tiles, 2)
        held_labels = held_labels.transpose(0, 2, 1, 3).reshape(slots, 2).astype(jnp.int32)
    else:
        held_emb = held[:, :width]
        held_labels = held[:, width : width + 2].astype(jnp.int32)

    index = jnp.arange(slots, dtype=jnp.int32)
    present = held_labels[:, 0] > 0
    source = index // capacity
    global_block = source * local_blocks + held_labels[:, 0] - 1
    global_block = jnp.where(present, global_block, 0)
    sub = jnp.where(present, held_labels[:, 1] - 1, -1 - index)
    block_count = cand.shape[1]
    block_onehot = (
        global_block[:, None] == jnp.arange(block_count, dtype=jnp.int32)[None, :]
    ).astype(jnp.bfloat16)
    cand_rows = jnp.dot(block_onehot, cand.astype(jnp.bfloat16), preferred_element_type=jnp.float32)
    near = (
        lax.dot_general(
            cand_rows.astype(jnp.bfloat16),
            block_onehot,
            (((1,), (1,)), ((), ())),
            preferred_element_type=jnp.float32,
        )
        > 0.5
    )
    averaged = attend(held_emb, near, sub)
    returned = lax.all_to_all(averaged, axes, split_axis=0, concat_axis=0, tiled=True)
    result = lax.dot_general(
        placing, returned, (((0,), (0,)), ((), ())), preferred_element_type=jnp.float32
    )
    return result.astype(jnp.bfloat16)


def solution(mesh):
    return jax.shard_map(
        body,
        mesh=mesh,
        in_specs=(
            P(("groups", "owner", "loop"), None),
            P(("groups", "owner", "loop")),
            P(("groups", "owner", "loop")),
            P("groups", None),
        ),
        out_specs=P(("groups", "owner", "loop"), None),
        check_vma=False,
    )
```

```python
import functools

import jax
import jax.numpy as jnp
from jax import lax
from jax.experimental import pallas as pl
from jax.experimental.pallas import tpu as pltpu
from jax.sharding import PartitionSpec as P

BLOCK = 128
SUB = 16
LABEL_COLUMNS = 128
TILE = 16


def place_kernel(
    emb_ref, owner_ref, sub_ref, send_ref, slot_ref, *, loop_count, capacity, devices, tiled
):
    rows, width = emb_ref.shape
    slots = devices * capacity
    owner = owner_ref[...]
    sub = sub_ref[...]
    dest = sub % loop_count * (devices // loop_count) + owner
    onehot_t = (lax.broadcasted_iota(jnp.int32, (devices, rows), 0) == dest).astype(jnp.bfloat16)
    upper = (
        lax.broadcasted_iota(jnp.int32, (rows, rows), 0)
        < lax.broadcasted_iota(jnp.int32, (rows, rows), 1)
    ).astype(jnp.bfloat16)
    earlier_t = jnp.dot(onehot_t, upper, preferred_element_type=jnp.float32)
    within = jnp.sum(earlier_t * onehot_t.astype(jnp.float32), axis=0, keepdims=True)
    slot = dest * capacity + within.astype(jnp.int32)
    slot_ref[...] = slot
    placing = (lax.broadcasted_iota(jnp.int32, (slots, rows), 0) == slot).astype(jnp.bfloat16)
    placed = jnp.dot(placing, emb_ref[...], preferred_element_type=jnp.float32).astype(
        send_ref.dtype
    )
    which = lax.broadcasted_iota(jnp.int32, (LABEL_COLUMNS, rows), 0)
    block = lax.broadcasted_iota(jnp.int32, (LABEL_COLUMNS, rows), 1) // BLOCK
    column = 0
    if tiled:
        column = slot % capacity // TILE * 2
    labels_t = jnp.where(which == column, block + 1, jnp.where(which == column + 1, sub + 1, 0))
    labels = labels_t.astype(jnp.float32).T.astype(jnp.bfloat16)
    placed_labels = jnp.dot(placing, labels, preferred_element_type=jnp.float32).astype(
        send_ref.dtype
    )
    if not tiled:
        send_ref[:, :width] = placed
        send_ref[:, width:] = placed_labels
        return
    row_tiles = capacity // TILE
    col_tiles = width // LABEL_COLUMNS
    for chunk in range(devices):
        base = chunk * capacity
        for a in range(row_tiles):
            for e in range(col_tiles):
                send_ref[chunk, (a * col_tiles + e) * TILE : (a * col_tiles + e + 1) * TILE, :] = placed[
                    base + a * TILE : base + (a + 1) * TILE, e * LABEL_COLUMNS : (e + 1) * LABEL_COLUMNS
                ]
        tile = placed_labels[base : base + TILE]
        for a in range(1, row_tiles):
            tile = tile + placed_labels[base + a * TILE : base + (a + 1) * TILE]
        send_ref[chunk, row_tiles * col_tiles * TILE :, :] = tile


def place(emb, row_owner, row_sub, loop_count, capacity, devices, tiled):
    rows, width = emb.shape
    slots = devices * capacity
    vmem = pl.BlockSpec(memory_space=pltpu.VMEM)
    cost = pl.CostEstimate(
        flops=2 * slots * rows * (width + LABEL_COLUMNS) + 2 * devices * rows * rows,
        transcendentals=0,
        bytes_accessed=rows * width * 2 + slots * (width + LABEL_COLUMNS) * 2,
    )
    if tiled:
        shape = (devices, capacity * width // LABEL_COLUMNS + TILE, LABEL_COLUMNS)
    else:
        shape = (slots, width + LABEL_COLUMNS)
    return pl.pallas_call(
        functools.partial(
            place_kernel, loop_count=loop_count, capacity=capacity, devices=devices, tiled=tiled
        ),
        out_shape=(
            jax.ShapeDtypeStruct(shape, jnp.bfloat16),
            jax.ShapeDtypeStruct((1, rows), jnp.int32),
        ),
        in_specs=[vmem] * 3,
        out_specs=(vmem, vmem),
        cost_estimate=cost,
    )(emb, row_owner[None, :], row_sub[None, :])


def attend(keys, near, sub):
    slots = keys.shape[0]
    scale = 4.0 / keys.shape[1]
    scores = scale * lax.dot_general(
        keys, keys, (((1,), (1,)), ((), ())), preferred_element_type=jnp.float32
    )
    index = jnp.arange(slots, dtype=jnp.int32)
    same = (index[:, None] == index[None, :]) | (
        (sub[:, None] == sub[None, :]) & near
    )
    top = jnp.max(jnp.where(same, scores, jnp.float32(-1e30)), axis=1)
    weights = jnp.where(same, jnp.exp(scores - top[:, None]), jnp.float32(0.0))
    total = jnp.sum(weights, axis=1)
    summed = jnp.dot(weights.astype(jnp.bfloat16), keys, preferred_element_type=jnp.float32)
    return (summed / total[:, None]).astype(jnp.bfloat16)


def body(emb, row_owner, row_sub, cand):
    rows = emb.shape[0]
    owner_count = lax.axis_size("owner")
    loop_count = lax.axis_size("loop")
    devices = owner_count * loop_count
    capacity = 2 * rows // owner_count // loop_count
    slots = devices * capacity
    local_blocks = rows // BLOCK
    axes = ("loop", "owner")

    width = emb.shape[1]
    tiled = capacity % TILE == 0 and width % LABEL_COLUMNS == 0
    send, slot_of_row = place(emb, row_owner, row_sub, loop_count, capacity, devices, tiled)
    slot_of_row = slot_of_row[0]
    placing = (jnp.arange(slots, dtype=jnp.int32)[:, None] == slot_of_row[None, :]).astype(
        jnp.bfloat16
    )
    held = lax.all_to_all(send, axes, split_axis=0, concat_axis=0, tiled=True)
    if tiled:
        row_tiles = capacity // TILE
        col_tiles = width // LABEL_COLUMNS
        body_rows = row_tiles * col_tiles * TILE
        held_emb = held[:, :body_rows].reshape(devices, row_tiles, col_tiles, TILE, LABEL_COLUMNS)
        held_emb = held_emb.transpose(0, 1, 3, 2, 4).reshape(slots, width)
        held_labels = held[:, body_rows:, : 2 * row_tiles].reshape(devices, TILE, row_tiles, 2)
        held_labels = held_labels.transpose(0, 2, 1, 3).reshape(slots, 2).astype(jnp.int32)
    else:
        held_emb = held[:, :width]
        held_labels = held[:, width : width + 2].astype(jnp.int32)

    index = jnp.arange(slots, dtype=jnp.int32)
    present = held_labels[:, 0] > 0
    source = index // capacity
    source = source % owner_count * loop_count + source // owner_count
    global_block = source * local_blocks + held_labels[:, 0] - 1
    global_block = jnp.where(present, global_block, 0)
    sub = jnp.where(present, held_labels[:, 1] - 1, -1 - index)
    block_count = cand.shape[1]
    block_onehot = (
        global_block[:, None] == jnp.arange(block_count, dtype=jnp.int32)[None, :]
    ).astype(jnp.bfloat16)
    cand_rows = jnp.dot(block_onehot, cand.astype(jnp.bfloat16), preferred_element_type=jnp.float32)
    near = (
        lax.dot_general(
            cand_rows.astype(jnp.bfloat16),
            block_onehot,
            (((1,), (1,)), ((), ())),
            preferred_element_type=jnp.float32,
        )
        > 0.5
    )
    averaged = attend(held_emb, near, sub)
    returned = lax.all_to_all(averaged, axes, split_axis=0, concat_axis=0, tiled=True)
    result = lax.dot_general(
        placing, returned, (((0,), (0,)), ((), ())), preferred_element_type=jnp.float32
    )
    return result.astype(jnp.bfloat16)


def solution(mesh):
    return jax.shard_map(
        body,
        mesh=mesh,
        in_specs=(
            P(("groups", "owner", "loop"), None),
            P(("groups", "owner", "loop")),
            P(("groups", "owner", "loop")),
            P("groups", None),
        ),
        out_specs=P(("groups", "owner", "loop"), None),
        check_vma=False,
    )
```

```python
import functools

import jax
import jax.numpy as jnp
from jax import lax
from jax.experimental import pallas as pl
from jax.experimental.pallas import tpu as pltpu
from jax.sharding import PartitionSpec as P

BLOCK = 128
SUB = 16
LABEL_COLUMNS = 128
TILE = 16


def place_kernel(
    emb_ref, owner_ref, sub_ref, send_ref, slot_ref, *, loop_count, capacity, devices, tiled
):
    rows, width = emb_ref.shape
    slots = devices * capacity
    owner = owner_ref[...]
    sub = sub_ref[...]
    dest = sub % loop_count * (devices // loop_count) + owner
    onehot_t = (lax.broadcasted_iota(jnp.int32, (devices, rows), 0) == dest).astype(jnp.bfloat16)
    upper = (
        lax.broadcasted_iota(jnp.int32, (rows, rows), 0)
        < lax.broadcasted_iota(jnp.int32, (rows, rows), 1)
    ).astype(jnp.bfloat16)
    earlier_t = jnp.dot(onehot_t, upper, preferred_element_type=jnp.float32)
    within = jnp.sum(earlier_t * onehot_t.astype(jnp.float32), axis=0, keepdims=True)
    slot = dest * capacity + within.astype(jnp.int32)
    slot_ref[...] = slot
    placing = (lax.broadcasted_iota(jnp.int32, (slots, rows), 0) == slot).astype(jnp.bfloat16)
    which = lax.broadcasted_iota(jnp.int32, (LABEL_COLUMNS, rows), 0)
    block = lax.broadcasted_iota(jnp.int32, (LABEL_COLUMNS, rows), 1) // BLOCK
    column = 0
    if tiled:
        column = slot % capacity // TILE * 2
    labels_t = jnp.where(which == column, block + 1, jnp.where(which == column + 1, sub + 1, 0))
    labels = labels_t.astype(jnp.float32).T.astype(jnp.bfloat16)
    placed_labels = jnp.dot(placing, labels, preferred_element_type=jnp.float32).astype(
        send_ref.dtype
    )
    if not tiled:
        send_ref[:, :width] = jnp.dot(
            placing, emb_ref[...], preferred_element_type=jnp.float32
        ).astype(send_ref.dtype)
        send_ref[:, width:] = placed_labels
        return
    row_tiles = capacity // TILE
    col_tiles = width // LABEL_COLUMNS
    for e in range(col_tiles):
        stripe = jnp.dot(
            placing,
            emb_ref[:, e * LABEL_COLUMNS : (e + 1) * LABEL_COLUMNS],
            preferred_element_type=jnp.float32,
        ).astype(send_ref.dtype)
        for chunk in range(devices):
            base = chunk * capacity
            for a in range(row_tiles):
                t = a * col_tiles + e
                send_ref[chunk, t * TILE : (t + 1) * TILE, :] = stripe[
                    base + a * TILE : base + (a + 1) * TILE
                ]
    for chunk in range(devices):
        base = chunk * capacity
        tile = placed_labels[base : base + TILE]
        for a in range(1, row_tiles):
            tile = tile + placed_labels[base + a * TILE : base + (a + 1) * TILE]
        send_ref[chunk, row_tiles * col_tiles * TILE :, :] = tile


def place(emb, row_owner, row_sub, loop_count, capacity, devices, tiled):
    rows, width = emb.shape
    slots = devices * capacity
    vmem = pl.BlockSpec(memory_space=pltpu.VMEM)
    cost = pl.CostEstimate(
        flops=2 * slots * rows * (width + LABEL_COLUMNS) + 2 * devices * rows * rows,
        transcendentals=0,
        bytes_accessed=rows * width * 2 + slots * (width + LABEL_COLUMNS) * 2,
    )
    if tiled:
        shape = (devices, capacity * width // LABEL_COLUMNS + TILE, LABEL_COLUMNS)
    else:
        shape = (slots, width + LABEL_COLUMNS)
    return pl.pallas_call(
        functools.partial(
            place_kernel, loop_count=loop_count, capacity=capacity, devices=devices, tiled=tiled
        ),
        out_shape=(
            jax.ShapeDtypeStruct(shape, jnp.bfloat16),
            jax.ShapeDtypeStruct((1, rows), jnp.int32),
        ),
        in_specs=[vmem] * 3,
        out_specs=(vmem, vmem),
        cost_estimate=cost,
    )(emb, row_owner[None, :], row_sub[None, :])


def attend(keys, near, sub):
    slots = keys.shape[0]
    scale = 4.0 / keys.shape[1]
    scores = scale * lax.dot_general(
        keys, keys, (((1,), (1,)), ((), ())), preferred_element_type=jnp.float32
    )
    index = jnp.arange(slots, dtype=jnp.int32)
    same = (index[:, None] == index[None, :]) | (
        (sub[:, None] == sub[None, :]) & near
    )
    top = jnp.max(jnp.where(same, scores, jnp.float32(-1e30)), axis=1)
    weights = jnp.where(same, jnp.exp(scores - top[:, None]), jnp.float32(0.0))
    total = jnp.sum(weights, axis=1)
    summed = jnp.dot(weights.astype(jnp.bfloat16), keys, preferred_element_type=jnp.float32)
    return (summed / total[:, None]).astype(jnp.bfloat16)


def body(emb, row_owner, row_sub, cand):
    rows = emb.shape[0]
    owner_count = lax.axis_size("owner")
    loop_count = lax.axis_size("loop")
    devices = owner_count * loop_count
    capacity = 2 * rows // owner_count // loop_count
    slots = devices * capacity
    local_blocks = rows // BLOCK
    axes = ("loop", "owner")

    width = emb.shape[1]
    tiled = capacity % TILE == 0 and width % LABEL_COLUMNS == 0
    send, slot_of_row = place(emb, row_owner, row_sub, loop_count, capacity, devices, tiled)
    slot_of_row = slot_of_row[0]
    placing = (jnp.arange(slots, dtype=jnp.int32)[:, None] == slot_of_row[None, :]).astype(
        jnp.bfloat16
    )
    held = lax.all_to_all(send, axes, split_axis=0, concat_axis=0, tiled=True)
    if tiled:
        row_tiles = capacity // TILE
        col_tiles = width // LABEL_COLUMNS
        body_rows = row_tiles * col_tiles * TILE
        held_emb = held[:, :body_rows].reshape(devices, row_tiles, col_tiles, TILE, LABEL_COLUMNS)
        held_emb = held_emb.transpose(0, 1, 3, 2, 4).reshape(slots, width)
        held_labels = held[:, body_rows:, : 2 * row_tiles].reshape(devices, TILE, row_tiles, 2)
        held_labels = held_labels.transpose(0, 2, 1, 3).reshape(slots, 2).astype(jnp.int32)
    else:
        held_emb = held[:, :width]
        held_labels = held[:, width : width + 2].astype(jnp.int32)

    index = jnp.arange(slots, dtype=jnp.int32)
    present = held_labels[:, 0] > 0
    source = index // capacity
    source = source % owner_count * loop_count + source // owner_count
    global_block = source * local_blocks + held_labels[:, 0] - 1
    global_block = jnp.where(present, global_block, 0)
    sub = jnp.where(present, held_labels[:, 1] - 1, -1 - index)
    block_count = cand.shape[1]
    block_onehot = (
        global_block[:, None] == jnp.arange(block_count, dtype=jnp.int32)[None, :]
    ).astype(jnp.bfloat16)
    cand_rows = jnp.dot(block_onehot, cand.astype(jnp.bfloat16), preferred_element_type=jnp.float32)
    near = (
        lax.dot_general(
            cand_rows.astype(jnp.bfloat16),
            block_onehot,
            (((1,), (1,)), ((), ())),
            preferred_element_type=jnp.float32,
        )
        > 0.5
    )
    averaged = attend(held_emb, near, sub)
    returned = lax.all_to_all(averaged, axes, split_axis=0, concat_axis=0, tiled=True)
    result = lax.dot_general(
        placing, returned, (((0,), (0,)), ((), ())), preferred_element_type=jnp.float32
    )
    return result.astype(jnp.bfloat16)


def solution(mesh):
    return jax.shard_map(
        body,
        mesh=mesh,
        in_specs=(
            P(("groups", "owner", "loop"), None),
            P(("groups", "owner", "loop")),
            P(("groups", "owner", "loop")),
            P("groups", None),
        ),
        out_specs=P(("groups", "owner", "loop"), None),
        check_vma=False,
    )
```

```python
import functools

import jax
import jax.numpy as jnp
from jax import lax
from jax.experimental import pallas as pl
from jax.experimental.pallas import tpu as pltpu
from jax.sharding import PartitionSpec as P

BLOCK = 128
SUB = 16
LABEL_COLUMNS = 128
TILE = 16


def place_kernel(
    emb_ref, owner_ref, sub_ref, send_ref, slot_ref, *, loop_count, capacity, devices, tiled
):
    rows, width = emb_ref.shape
    slots = devices * capacity
    owner = owner_ref[...]
    sub = sub_ref[...]
    dest = sub % loop_count * (devices // loop_count) + owner
    onehot_t = (lax.broadcasted_iota(jnp.int32, (devices, rows), 0) == dest).astype(jnp.bfloat16)
    upper = (
        lax.broadcasted_iota(jnp.int32, (rows, rows), 0)
        < lax.broadcasted_iota(jnp.int32, (rows, rows), 1)
    ).astype(jnp.bfloat16)
    earlier_t = jnp.dot(onehot_t, upper, preferred_element_type=jnp.float32)
    within = jnp.sum(earlier_t * onehot_t.astype(jnp.float32), axis=0, keepdims=True)
    slot = dest * capacity + within.astype(jnp.int32)
    slot_ref[...] = slot
    placing = (lax.broadcasted_iota(jnp.int32, (slots, rows), 0) == slot).astype(jnp.bfloat16)
    placed = jnp.dot(placing, emb_ref[...], preferred_element_type=jnp.float32).astype(
        send_ref.dtype
    )
    which = lax.broadcasted_iota(jnp.int32, (LABEL_COLUMNS, rows), 0)
    block = lax.broadcasted_iota(jnp.int32, (LABEL_COLUMNS, rows), 1) // BLOCK
    column = 0
    if tiled:
        column = slot % capacity // TILE * 2
    labels_t = jnp.where(which == column, block + 1, jnp.where(which == column + 1, sub + 1, 0))
    labels = labels_t.astype(jnp.float32).T.astype(jnp.bfloat16)
    placed_labels = jnp.dot(placing, labels, preferred_element_type=jnp.float32).astype(
        send_ref.dtype
    )
    if not tiled:
        send_ref[:, :width] = placed
        send_ref[:, width:] = placed_labels
        return
    row_tiles = capacity // TILE
    col_tiles = width // LABEL_COLUMNS
    for chunk in range(devices):
        base = chunk * capacity
        for a in range(row_tiles):
            for e in range(col_tiles):
                send_ref[chunk, (a * col_tiles + e) * TILE : (a * col_tiles + e + 1) * TILE, :] = placed[
                    base + a * TILE : base + (a + 1) * TILE, e * LABEL_COLUMNS : (e + 1) * LABEL_COLUMNS
                ]
        tile = placed_labels[base : base + TILE]
        for a in range(1, row_tiles):
            tile = tile + placed_labels[base + a * TILE : base + (a + 1) * TILE]
        send_ref[chunk, row_tiles * col_tiles * TILE :, :] = tile


def place(emb, row_owner, row_sub, loop_count, capacity, devices, tiled):
    rows, width = emb.shape
    slots = devices * capacity
    vmem = pl.BlockSpec(memory_space=pltpu.VMEM)
    cost = pl.CostEstimate(
        flops=2 * slots * rows * (width + LABEL_COLUMNS) + 2 * devices * rows * rows,
        transcendentals=0,
        bytes_accessed=rows * width * 2 + slots * (width + LABEL_COLUMNS) * 2,
    )
    if tiled:
        shape = (devices, capacity * width // LABEL_COLUMNS + TILE, LABEL_COLUMNS)
    else:
        shape = (slots, width + LABEL_COLUMNS)
    return pl.pallas_call(
        functools.partial(
            place_kernel, loop_count=loop_count, capacity=capacity, devices=devices, tiled=tiled
        ),
        out_shape=(
            jax.ShapeDtypeStruct(shape, jnp.bfloat16),
            jax.ShapeDtypeStruct((1, rows), jnp.int32),
        ),
        in_specs=[vmem] * 3,
        out_specs=(vmem, vmem),
        cost_estimate=cost,
    )(emb, row_owner[None, :], row_sub[None, :])


def attend(keys, near, sub):
    slots = keys.shape[0]
    scale = 4.0 / keys.shape[1]
    scores = scale * lax.dot_general(
        keys, keys, (((1,), (1,)), ((), ())), preferred_element_type=jnp.float32
    )
    index = jnp.arange(slots, dtype=jnp.int32)
    same = (index[:, None] == index[None, :]) | (
        (sub[:, None] == sub[None, :]) & near
    )
    top = jnp.max(jnp.where(same, scores, jnp.float32(-1e30)), axis=1)
    weights = jnp.where(same, jnp.exp(scores - top[:, None]), jnp.float32(0.0))
    total = jnp.sum(weights, axis=1)
    summed = jnp.dot(weights.astype(jnp.bfloat16), keys, preferred_element_type=jnp.float32)
    return (summed / total[:, None]).astype(jnp.bfloat16)


def body(emb, row_owner, row_sub, cand):
    rows = emb.shape[0]
    owner_count = lax.axis_size("owner")
    loop_count = lax.axis_size("loop")
    devices = owner_count * loop_count
    capacity = 2 * rows // owner_count // loop_count
    slots = devices * capacity
    local_blocks = rows // BLOCK
    axes = ("loop", "owner")

    width = emb.shape[1]
    tiled = False
    send, slot_of_row = place(emb, row_owner, row_sub, loop_count, capacity, devices, tiled)
    slot_of_row = slot_of_row[0]
    placing = (jnp.arange(slots, dtype=jnp.int32)[:, None] == slot_of_row[None, :]).astype(
        jnp.bfloat16
    )
    held = lax.all_to_all(send, axes, split_axis=0, concat_axis=0, tiled=True)
    if tiled:
        row_tiles = capacity // TILE
        col_tiles = width // LABEL_COLUMNS
        body_rows = row_tiles * col_tiles * TILE
        held_emb = held[:, :body_rows].reshape(devices, row_tiles, col_tiles, TILE, LABEL_COLUMNS)
        held_emb = held_emb.transpose(0, 1, 3, 2, 4).reshape(slots, width)
        held_labels = held[:, body_rows:, : 2 * row_tiles].reshape(devices, TILE, row_tiles, 2)
        held_labels = held_labels.transpose(0, 2, 1, 3).reshape(slots, 2).astype(jnp.int32)
    else:
        held_emb = held[:, :width]
        held_labels = held[:, width : width + 2].astype(jnp.int32)

    index = jnp.arange(slots, dtype=jnp.int32)
    present = held_labels[:, 0] > 0
    source = index // capacity
    source = source % owner_count * loop_count + source // owner_count
    global_block = source * local_blocks + held_labels[:, 0] - 1
    global_block = jnp.where(present, global_block, 0)
    sub = jnp.where(present, held_labels[:, 1] - 1, -1 - index)
    block_count = cand.shape[1]
    block_onehot = (
        global_block[:, None] == jnp.arange(block_count, dtype=jnp.int32)[None, :]
    ).astype(jnp.bfloat16)
    cand_rows = jnp.dot(block_onehot, cand.astype(jnp.bfloat16), preferred_element_type=jnp.float32)
    near = (
        lax.dot_general(
            cand_rows.astype(jnp.bfloat16),
            block_onehot,
            (((1,), (1,)), ((), ())),
            preferred_element_type=jnp.float32,
        )
        > 0.5
    )
    averaged = attend(held_emb, near, sub)
    returned = lax.all_to_all(averaged, axes, split_axis=0, concat_axis=0, tiled=True)
    result = lax.dot_general(
        placing, returned, (((0,), (0,)), ((), ())), preferred_element_type=jnp.float32
    )
    return result.astype(jnp.bfloat16)


def solution(mesh):
    return jax.shard_map(
        body,
        mesh=mesh,
        in_specs=(
            P(("groups", "owner", "loop"), None),
            P(("groups", "owner", "loop")),
            P(("groups", "owner", "loop")),
            P("groups", None),
        ),
        out_specs=P(("groups", "owner", "loop"), None),
        check_vma=False,
    )
```

```python
import functools

import jax
import jax.numpy as jnp
from jax import lax
from jax.experimental import pallas as pl
from jax.experimental.pallas import tpu as pltpu
from jax.sharding import PartitionSpec as P

BLOCK = 128
SUB = 16
LABEL_COLUMNS = 128
TILE = 16


def place_kernel(
    emb_ref, owner_ref, sub_ref, send_ref, slot_ref, *, loop_count, capacity, devices, tiled
):
    rows, width = emb_ref.shape
    slots = devices * capacity
    owner = owner_ref[...]
    sub = sub_ref[...]
    dest = sub % loop_count * (devices // loop_count) + owner
    onehot_t = (lax.broadcasted_iota(jnp.int32, (devices, rows), 0) == dest).astype(jnp.bfloat16)
    upper = (
        lax.broadcasted_iota(jnp.int32, (rows, rows), 0)
        < lax.broadcasted_iota(jnp.int32, (rows, rows), 1)
    ).astype(jnp.bfloat16)
    earlier_t = jnp.dot(onehot_t, upper, preferred_element_type=jnp.float32)
    within = jnp.sum(earlier_t * onehot_t.astype(jnp.float32), axis=0, keepdims=True)
    slot = dest * capacity + within.astype(jnp.int32)
    slot_ref[...] = slot
    placing = (lax.broadcasted_iota(jnp.int32, (slots, rows), 0) == slot).astype(jnp.bfloat16)
    placed = jnp.dot(placing, emb_ref[...], preferred_element_type=jnp.float32).astype(
        send_ref.dtype
    )
    if not tiled:
        which = lax.broadcasted_iota(jnp.int32, (LABEL_COLUMNS, rows), 0)
        block = lax.broadcasted_iota(jnp.int32, (LABEL_COLUMNS, rows), 1) // BLOCK
        labels_t = jnp.where(which == 0, block + 1, jnp.where(which == 1, sub + 1, 0))
        labels = labels_t.astype(jnp.float32).T.astype(jnp.bfloat16)
        placed_labels = jnp.dot(placing, labels, preferred_element_type=jnp.float32).astype(
            send_ref.dtype
        )
        send_ref[:, :width] = placed
        send_ref[:, width:] = placed_labels
        return
    row_tiles = capacity // TILE
    col_tiles = width // LABEL_COLUMNS
    which = lax.broadcasted_iota(jnp.int32, (8, rows), 0)
    block = lax.broadcasted_iota(jnp.int32, (8, rows), 1) // BLOCK
    labels_rows = jnp.where(which == 0, block + 1, jnp.where(which == 1, sub + 1, 0))
    placed_rows = lax.dot_general(
        labels_rows.astype(jnp.float32).astype(jnp.bfloat16),
        placing,
        (((1,), (1,)), ((), ())),
        preferred_element_type=jnp.float32,
    ).astype(send_ref.dtype)
    body_rows = row_tiles * col_tiles * TILE
    per_lanes = LABEL_COLUMNS // capacity
    for chunk in range(devices):
        base = chunk * capacity
        for a in range(row_tiles):
            for e in range(col_tiles):
                send_ref[chunk, (a * col_tiles + e) * TILE : (a * col_tiles + e + 1) * TILE, :] = placed[
                    base + a * TILE : base + (a + 1) * TILE, e * LABEL_COLUMNS : (e + 1) * LABEL_COLUMNS
                ]
        lanes = chunk // per_lanes * LABEL_COLUMNS
        send_ref[chunk, body_rows : body_rows + 8, :] = placed_rows[:, lanes : lanes + LABEL_COLUMNS]
        send_ref[chunk, body_rows + 8 :, :] = jnp.zeros((TILE - 8, LABEL_COLUMNS), send_ref.dtype)


def place(emb, row_owner, row_sub, loop_count, capacity, devices, tiled):
    rows, width = emb.shape
    slots = devices * capacity
    vmem = pl.BlockSpec(memory_space=pltpu.VMEM)
    cost = pl.CostEstimate(
        flops=2 * slots * rows * (width + LABEL_COLUMNS) + 2 * devices * rows * rows,
        transcendentals=0,
        bytes_accessed=rows * width * 2 + slots * (width + LABEL_COLUMNS) * 2,
    )
    if tiled:
        shape = (devices, capacity * width // LABEL_COLUMNS + TILE, LABEL_COLUMNS)
    else:
        shape = (slots, width + LABEL_COLUMNS)
    return pl.pallas_call(
        functools.partial(
            place_kernel, loop_count=loop_count, capacity=capacity, devices=devices, tiled=tiled
        ),
        out_shape=(
            jax.ShapeDtypeStruct(shape, jnp.bfloat16),
            jax.ShapeDtypeStruct((1, rows), jnp.int32),
        ),
        in_specs=[vmem] * 3,
        out_specs=(vmem, vmem),
        cost_estimate=cost,
    )(emb, row_owner[None, :], row_sub[None, :])


def attend(keys, near, sub):
    slots = keys.shape[0]
    scale = 4.0 / keys.shape[1]
    scores = scale * lax.dot_general(
        keys, keys, (((1,), (1,)), ((), ())), preferred_element_type=jnp.float32
    )
    index = jnp.arange(slots, dtype=jnp.int32)
    same = (index[:, None] == index[None, :]) | (
        (sub[:, None] == sub[None, :]) & near
    )
    top = jnp.max(jnp.where(same, scores, jnp.float32(-1e30)), axis=1)
    weights = jnp.where(same, jnp.exp(scores - top[:, None]), jnp.float32(0.0))
    total = jnp.sum(weights, axis=1)
    summed = jnp.dot(weights.astype(jnp.bfloat16), keys, preferred_element_type=jnp.float32)
    return (summed / total[:, None]).astype(jnp.bfloat16)


def body(emb, row_owner, row_sub, cand):
    rows = emb.shape[0]
    owner_count = lax.axis_size("owner")
    loop_count = lax.axis_size("loop")
    devices = owner_count * loop_count
    capacity = 2 * rows // owner_count // loop_count
    slots = devices * capacity
    local_blocks = rows // BLOCK
    axes = ("loop", "owner")

    width = emb.shape[1]
    tiled = capacity % TILE == 0 and width % LABEL_COLUMNS == 0 and LABEL_COLUMNS % capacity == 0
    send, slot_of_row = place(emb, row_owner, row_sub, loop_count, capacity, devices, tiled)
    slot_of_row = slot_of_row[0]
    placing = (jnp.arange(slots, dtype=jnp.int32)[:, None] == slot_of_row[None, :]).astype(
        jnp.bfloat16
    )
    held = lax.all_to_all(send, axes, split_axis=0, concat_axis=0, tiled=True)
    if tiled:
        row_tiles = capacity // TILE
        col_tiles = width // LABEL_COLUMNS
        body_rows = row_tiles * col_tiles * TILE
        held_emb = held[:, :body_rows].reshape(devices, row_tiles, col_tiles, TILE, LABEL_COLUMNS)
        held_emb = held_emb.transpose(0, 1, 3, 2, 4).reshape(slots, width)
        per_lanes = LABEL_COLUMNS // capacity
        lanes = held[:, body_rows : body_rows + 2, :].reshape(devices, 2, per_lanes, capacity)
        me = lax.axis_index("loop") * owner_count + lax.axis_index("owner")
        held_labels = lax.dynamic_index_in_dim(lanes, me % per_lanes, axis=2, keepdims=False)
        held_labels = held_labels.astype(jnp.int32).transpose(0, 2, 1).reshape(slots, 2)
    else:
        held_emb = held[:, :width]
        held_labels = held[:, width : width + 2].astype(jnp.int32)

    index = jnp.arange(slots, dtype=jnp.int32)
    present = held_labels[:, 0] > 0
    source = index // capacity
    source = source % owner_count * loop_count + source // owner_count
    global_block = source * local_blocks + held_labels[:, 0] - 1
    global_block = jnp.where(present, global_block, 0)
    sub = jnp.where(present, held_labels[:, 1] - 1, -1 - index)
    block_count = cand.shape[1]
    block_onehot = (
        global_block[:, None] == jnp.arange(block_count, dtype=jnp.int32)[None, :]
    ).astype(jnp.bfloat16)
    cand_rows = jnp.dot(block_onehot, cand.astype(jnp.bfloat16), preferred_element_type=jnp.float32)
    near = (
        lax.dot_general(
            cand_rows.astype(jnp.bfloat16),
            block_onehot,
            (((1,), (1,)), ((), ())),
            preferred_element_type=jnp.float32,
        )
        > 0.5
    )
    averaged = attend(held_emb, near, sub)
    returned = lax.all_to_all(averaged, axes, split_axis=0, concat_axis=0, tiled=True)
    result = lax.dot_general(
        placing, returned, (((0,), (0,)), ((), ())), preferred_element_type=jnp.float32
    )
    return result.astype(jnp.bfloat16)


def solution(mesh):
    return jax.shard_map(
        body,
        mesh=mesh,
        in_specs=(
            P(("groups", "owner", "loop"), None),
            P(("groups", "owner", "loop")),
            P(("groups", "owner", "loop")),
            P("groups", None),
        ),
        out_specs=P(("groups", "owner", "loop"), None),
        check_vma=False,
    )
```

```python
import functools

import jax
import jax.numpy as jnp
from jax import lax
from jax.experimental import pallas as pl
from jax.experimental.pallas import tpu as pltpu
from jax.sharding import PartitionSpec as P

BLOCK = 128
SUB = 16
LABEL_COLUMNS = 128
TILE = 16


def place_kernel(
    emb_ref, owner_ref, sub_ref, send_ref, slot_ref, *, loop_count, capacity, devices, tiled
):
    rows, width = emb_ref.shape
    slots = devices * capacity
    owner = owner_ref[...]
    sub = sub_ref[...]
    dest = sub % loop_count * (devices // loop_count) + owner
    onehot_t = (lax.broadcasted_iota(jnp.int32, (devices, rows), 0) == dest).astype(jnp.bfloat16)
    upper = (
        lax.broadcasted_iota(jnp.int32, (rows, rows), 0)
        < lax.broadcasted_iota(jnp.int32, (rows, rows), 1)
    ).astype(jnp.bfloat16)
    earlier_t = jnp.dot(onehot_t, upper, preferred_element_type=jnp.float32)
    within = jnp.sum(earlier_t * onehot_t.astype(jnp.float32), axis=0, keepdims=True)
    slot = dest * capacity + within.astype(jnp.int32)
    slot_ref[...] = slot
    placing = (lax.broadcasted_iota(jnp.int32, (slots, rows), 0) == slot).astype(jnp.bfloat16)
    placed = jnp.dot(placing, emb_ref[...], preferred_element_type=jnp.float32).astype(
        send_ref.dtype
    )
    if not tiled:
        which = lax.broadcasted_iota(jnp.int32, (LABEL_COLUMNS, rows), 0)
        block = lax.broadcasted_iota(jnp.int32, (LABEL_COLUMNS, rows), 1) // BLOCK
        labels_t = jnp.where(which == 0, block + 1, jnp.where(which == 1, sub + 1, 0))
        labels = labels_t.astype(jnp.float32).T.astype(jnp.bfloat16)
        placed_labels = jnp.dot(placing, labels, preferred_element_type=jnp.float32).astype(
            send_ref.dtype
        )
        send_ref[:, :width] = placed
        send_ref[:, width:] = placed_labels
        return
    row_tiles = capacity // TILE
    col_tiles = width // LABEL_COLUMNS
    which = lax.broadcasted_iota(jnp.int32, (8, rows), 0)
    block = lax.broadcasted_iota(jnp.int32, (8, rows), 1) // BLOCK
    labels_rows = jnp.where(which == 0, block + 1, jnp.where(which == 1, sub + 1, 0))
    placed_rows = lax.dot_general(
        labels_rows.astype(jnp.float32).astype(jnp.bfloat16),
        placing,
        (((1,), (1,)), ((), ())),
        preferred_element_type=jnp.float32,
    ).astype(send_ref.dtype)
    body_rows = row_tiles * col_tiles * TILE
    per_lanes = LABEL_COLUMNS // capacity
    for chunk in range(devices):
        base = chunk * capacity
        for a in range(row_tiles):
            for e in range(col_tiles):
                send_ref[chunk, (a * col_tiles + e) * TILE : (a * col_tiles + e + 1) * TILE, :] = placed[
                    base + a * TILE : base + (a + 1) * TILE, e * LABEL_COLUMNS : (e + 1) * LABEL_COLUMNS
                ]
        lanes = chunk // per_lanes * LABEL_COLUMNS
        send_ref[chunk, body_rows : body_rows + 8, :] = placed_rows[:, lanes : lanes + LABEL_COLUMNS]
        send_ref[chunk, body_rows + 8 :, :] = jnp.zeros((TILE - 8, LABEL_COLUMNS), send_ref.dtype)


def place(emb, row_owner, row_sub, loop_count, capacity, devices, tiled):
    rows, width = emb.shape
    slots = devices * capacity
    vmem = pl.BlockSpec(memory_space=pltpu.VMEM)
    cost = pl.CostEstimate(
        flops=2 * slots * rows * (width + LABEL_COLUMNS) + 2 * devices * rows * rows,
        transcendentals=0,
        bytes_accessed=rows * width * 2 + slots * (width + LABEL_COLUMNS) * 2,
    )
    if tiled:
        shape = (devices, capacity * width // LABEL_COLUMNS + TILE, LABEL_COLUMNS)
    else:
        shape = (slots, width + LABEL_COLUMNS)
    return pl.pallas_call(
        functools.partial(
            place_kernel, loop_count=loop_count, capacity=capacity, devices=devices, tiled=tiled
        ),
        out_shape=(
            jax.ShapeDtypeStruct(shape, jnp.bfloat16),
            jax.ShapeDtypeStruct((1, rows), jnp.int32),
        ),
        in_specs=[vmem] * 3,
        out_specs=(vmem, vmem),
        cost_estimate=cost,
    )(emb, row_owner[None, :], row_sub[None, :])


def attend(keys, near, sub):
    slots = keys.shape[0]
    scale = 4.0 / keys.shape[1]
    scores = scale * lax.dot_general(
        keys, keys, (((1,), (1,)), ((), ())), preferred_element_type=jnp.float32
    )
    index = jnp.arange(slots, dtype=jnp.int32)
    same = (index[:, None] == index[None, :]) | (
        (sub[:, None] == sub[None, :]) & near
    )
    top = jnp.max(jnp.where(same, scores, jnp.float32(-1e30)), axis=1)
    weights = jnp.where(same, jnp.exp(scores - top[:, None]), jnp.float32(0.0))
    total = jnp.sum(weights, axis=1)
    summed = jnp.dot(weights.astype(jnp.bfloat16), keys, preferred_element_type=jnp.float32)
    return (summed / total[:, None]).astype(jnp.bfloat16)


def body(emb, row_owner, row_sub, cand):
    rows = emb.shape[0]
    owner_count = lax.axis_size("owner")
    loop_count = lax.axis_size("loop")
    devices = owner_count * loop_count
    capacity = 2 * rows // owner_count // loop_count
    slots = devices * capacity
    local_blocks = rows // BLOCK
    axes = ("loop", "owner")

    width = emb.shape[1]
    tiled = capacity % TILE == 0 and width % LABEL_COLUMNS == 0 and LABEL_COLUMNS % capacity == 0
    send, slot_of_row = place(emb, row_owner, row_sub, loop_count, capacity, devices, tiled)
    slot_of_row = slot_of_row[0]
    placing = (jnp.arange(slots, dtype=jnp.int32)[:, None] == slot_of_row[None, :]).astype(
        jnp.bfloat16
    )
    placing = lax.optimization_barrier(placing)
    held = lax.all_to_all(send, axes, split_axis=0, concat_axis=0, tiled=True)
    if tiled:
        row_tiles = capacity // TILE
        col_tiles = width // LABEL_COLUMNS
        body_rows = row_tiles * col_tiles * TILE
        held_emb = held[:, :body_rows].reshape(devices, row_tiles, col_tiles, TILE, LABEL_COLUMNS)
        held_emb = held_emb.transpose(0, 1, 3, 2, 4).reshape(slots, width)
        per_lanes = LABEL_COLUMNS // capacity
        lanes = held[:, body_rows : body_rows + 2, :].reshape(devices, 2, per_lanes, capacity)
        me = lax.axis_index("loop") * owner_count + lax.axis_index("owner")
        held_labels = lax.dynamic_index_in_dim(lanes, me % per_lanes, axis=2, keepdims=False)
        held_labels = held_labels.astype(jnp.int32).transpose(0, 2, 1).reshape(slots, 2)
    else:
        held_emb = held[:, :width]
        held_labels = held[:, width : width + 2].astype(jnp.int32)

    index = jnp.arange(slots, dtype=jnp.int32)
    present = held_labels[:, 0] > 0
    source = index // capacity
    source = source % owner_count * loop_count + source // owner_count
    global_block = source * local_blocks + held_labels[:, 0] - 1
    global_block = jnp.where(present, global_block, 0)
    sub = jnp.where(present, held_labels[:, 1] - 1, -1 - index)
    block_count = cand.shape[1]
    block_onehot = (
        global_block[:, None] == jnp.arange(block_count, dtype=jnp.int32)[None, :]
    ).astype(jnp.bfloat16)
    cand_rows = jnp.dot(block_onehot, cand.astype(jnp.bfloat16), preferred_element_type=jnp.float32)
    near = (
        lax.dot_general(
            cand_rows.astype(jnp.bfloat16),
            block_onehot,
            (((1,), (1,)), ((), ())),
            preferred_element_type=jnp.float32,
        )
        > 0.5
    )
    averaged = attend(held_emb, near, sub)
    returned = lax.all_to_all(averaged, axes, split_axis=0, concat_axis=0, tiled=True)
    result = lax.dot_general(
        placing, returned, (((0,), (0,)), ((), ())), preferred_element_type=jnp.float32
    )
    return result.astype(jnp.bfloat16)


def solution(mesh):
    return jax.shard_map(
        body,
        mesh=mesh,
        in_specs=(
            P(("groups", "owner", "loop"), None),
            P(("groups", "owner", "loop")),
            P(("groups", "owner", "loop")),
            P("groups", None),
        ),
        out_specs=P(("groups", "owner", "loop"), None),
        check_vma=False,
    )
```

```python
import functools

import jax
import jax.numpy as jnp
from jax import lax
from jax.experimental import pallas as pl
from jax.experimental.pallas import tpu as pltpu
from jax.sharding import PartitionSpec as P

BLOCK = 128
SUB = 16
LABEL_COLUMNS = 128
TILE = 16


def place_kernel(
    emb_ref, owner_ref, sub_ref, send_ref, slot_ref, *, loop_count, capacity, devices, tiled
):
    rows, width = emb_ref.shape
    slots = devices * capacity
    owner = owner_ref[...]
    sub = sub_ref[...]
    dest = sub % loop_count * (devices // loop_count) + owner
    onehot_t = (lax.broadcasted_iota(jnp.int32, (devices, rows), 0) == dest).astype(jnp.bfloat16)
    upper = (
        lax.broadcasted_iota(jnp.int32, (rows, rows), 0)
        < lax.broadcasted_iota(jnp.int32, (rows, rows), 1)
    ).astype(jnp.bfloat16)
    earlier_t = jnp.dot(onehot_t, upper, preferred_element_type=jnp.float32)
    within = jnp.sum(earlier_t * onehot_t.astype(jnp.float32), axis=0, keepdims=True)
    slot = dest * capacity + within.astype(jnp.int32)
    slot_ref[...] = slot
    placing = (lax.broadcasted_iota(jnp.int32, (slots, rows), 0) == slot).astype(jnp.bfloat16)
    placed = jnp.dot(placing, emb_ref[...], preferred_element_type=jnp.float32).astype(
        send_ref.dtype
    )
    if not tiled:
        which = lax.broadcasted_iota(jnp.int32, (LABEL_COLUMNS, rows), 0)
        block = lax.broadcasted_iota(jnp.int32, (LABEL_COLUMNS, rows), 1) // BLOCK
        labels_t = jnp.where(which == 0, block + 1, jnp.where(which == 1, sub + 1, 0))
        labels = labels_t.astype(jnp.float32).T.astype(jnp.bfloat16)
        placed_labels = jnp.dot(placing, labels, preferred_element_type=jnp.float32).astype(
            send_ref.dtype
        )
        send_ref[:, :width] = placed
        send_ref[:, width:] = placed_labels
        return
    row_tiles = capacity // TILE
    col_tiles = width // LABEL_COLUMNS
    which = lax.broadcasted_iota(jnp.int32, (8, rows), 0)
    block = lax.broadcasted_iota(jnp.int32, (8, rows), 1) // BLOCK
    labels_rows = jnp.where(which == 0, block + 1, jnp.where(which == 1, sub + 1, 0))
    placed_rows = lax.dot_general(
        labels_rows.astype(jnp.float32).astype(jnp.bfloat16),
        placing,
        (((1,), (1,)), ((), ())),
        preferred_element_type=jnp.float32,
    ).astype(send_ref.dtype)
    body_rows = row_tiles * col_tiles * TILE
    per_lanes = LABEL_COLUMNS // capacity
    for chunk in range(devices):
        base = chunk * capacity
        for a in range(row_tiles):
            for e in range(col_tiles):
                send_ref[chunk, (a * col_tiles + e) * TILE : (a * col_tiles + e + 1) * TILE, :] = placed[
                    base + a * TILE : base + (a + 1) * TILE, e * LABEL_COLUMNS : (e + 1) * LABEL_COLUMNS
                ]
        lanes = chunk // per_lanes * LABEL_COLUMNS
        send_ref[chunk, body_rows : body_rows + 8, :] = placed_rows[:, lanes : lanes + LABEL_COLUMNS]
        send_ref[chunk, body_rows + 8 :, :] = jnp.zeros((TILE - 8, LABEL_COLUMNS), send_ref.dtype)


def place(emb, row_owner, row_sub, loop_count, capacity, devices, tiled):
    rows, width = emb.shape
    slots = devices * capacity
    vmem = pl.BlockSpec(memory_space=pltpu.VMEM)
    cost = pl.CostEstimate(
        flops=2 * slots * rows * (width + LABEL_COLUMNS) + 2 * devices * rows * rows,
        transcendentals=0,
        bytes_accessed=rows * width * 2 + slots * (width + LABEL_COLUMNS) * 2,
    )
    if tiled:
        shape = (devices, capacity * width // LABEL_COLUMNS + TILE, LABEL_COLUMNS)
    else:
        shape = (slots, width + LABEL_COLUMNS)
    return pl.pallas_call(
        functools.partial(
            place_kernel, loop_count=loop_count, capacity=capacity, devices=devices, tiled=tiled
        ),
        out_shape=(
            jax.ShapeDtypeStruct(shape, jnp.bfloat16),
            jax.ShapeDtypeStruct((1, rows), jnp.int32),
        ),
        in_specs=[vmem] * 3,
        out_specs=(vmem, vmem),
        cost_estimate=cost,
    )(emb, row_owner[None, :], row_sub[None, :])


def attend(keys, near, sub):
    slots = keys.shape[0]
    scale = 4.0 / keys.shape[1]
    scores = scale * lax.dot_general(
        keys, keys, (((1,), (1,)), ((), ())), preferred_element_type=jnp.float32
    )
    index = jnp.arange(slots, dtype=jnp.int32)
    same = (index[:, None] == index[None, :]) | (
        (sub[:, None] == sub[None, :]) & near
    )
    top = jnp.max(jnp.where(same, scores, jnp.float32(-1e30)), axis=1)
    weights = jnp.where(same, jnp.exp(scores - top[:, None]), jnp.float32(0.0))
    total = jnp.sum(weights, axis=1)
    summed = jnp.dot(weights.astype(jnp.bfloat16), keys, preferred_element_type=jnp.float32)
    return (summed / total[:, None]).astype(jnp.bfloat16)


def body(emb, row_owner, row_sub, cand):
    rows = emb.shape[0]
    owner_count = lax.axis_size("owner")
    loop_count = lax.axis_size("loop")
    devices = owner_count * loop_count
    capacity = 2 * rows // owner_count // loop_count
    slots = devices * capacity
    local_blocks = rows // BLOCK
    axes = ("loop", "owner")

    width = emb.shape[1]
    tiled = capacity % TILE == 0 and width % LABEL_COLUMNS == 0 and LABEL_COLUMNS % capacity == 0
    send, slot_of_row = place(emb, row_owner, row_sub, loop_count, capacity, devices, tiled)
    slot_of_row = slot_of_row[0]
    gathering = (slot_of_row[:, None] == jnp.arange(slots, dtype=jnp.int32)[None, :]).astype(
        jnp.bfloat16
    )
    held = lax.all_to_all(send, axes, split_axis=0, concat_axis=0, tiled=True)
    if tiled:
        row_tiles = capacity // TILE
        col_tiles = width // LABEL_COLUMNS
        body_rows = row_tiles * col_tiles * TILE
        held_emb = held[:, :body_rows].reshape(devices, row_tiles, col_tiles, TILE, LABEL_COLUMNS)
        held_emb = held_emb.transpose(0, 1, 3, 2, 4).reshape(slots, width)
        per_lanes = LABEL_COLUMNS // capacity
        lanes = held[:, body_rows : body_rows + 2, :].reshape(devices, 2, per_lanes, capacity)
        me = lax.axis_index("loop") * owner_count + lax.axis_index("owner")
        held_labels = lax.dynamic_index_in_dim(lanes, me % per_lanes, axis=2, keepdims=False)
        held_labels = held_labels.astype(jnp.int32).transpose(0, 2, 1).reshape(slots, 2)
    else:
        held_emb = held[:, :width]
        held_labels = held[:, width : width + 2].astype(jnp.int32)

    index = jnp.arange(slots, dtype=jnp.int32)
    present = held_labels[:, 0] > 0
    source = index // capacity
    source = source % owner_count * loop_count + source // owner_count
    global_block = source * local_blocks + held_labels[:, 0] - 1
    global_block = jnp.where(present, global_block, 0)
    sub = jnp.where(present, held_labels[:, 1] - 1, -1 - index)
    block_count = cand.shape[1]
    block_onehot = (
        global_block[:, None] == jnp.arange(block_count, dtype=jnp.int32)[None, :]
    ).astype(jnp.bfloat16)
    cand_rows = jnp.dot(block_onehot, cand.astype(jnp.bfloat16), preferred_element_type=jnp.float32)
    near = (
        lax.dot_general(
            cand_rows.astype(jnp.bfloat16),
            block_onehot,
            (((1,), (1,)), ((), ())),
            preferred_element_type=jnp.float32,
        )
        > 0.5
    )
    averaged = attend(held_emb, near, sub)
    returned = lax.all_to_all(averaged, axes, split_axis=0, concat_axis=0, tiled=True)
    result = jnp.dot(gathering, returned, preferred_element_type=jnp.float32)
    return result.astype(jnp.bfloat16)


def solution(mesh):
    return jax.shard_map(
        body,
        mesh=mesh,
        in_specs=(
            P(("groups", "owner", "loop"), None),
            P(("groups", "owner", "loop")),
            P(("groups", "owner", "loop")),
            P("groups", None),
        ),
        out_specs=P(("groups", "owner", "loop"), None),
        check_vma=False,
    )
```

```python
import functools

import jax
import jax.numpy as jnp
from jax import lax
from jax.experimental import pallas as pl
from jax.experimental.pallas import tpu as pltpu
from jax.sharding import PartitionSpec as P

BLOCK = 128
SUB = 16
LABEL_COLUMNS = 128
TILE = 16


def place_kernel(
    emb_ref, owner_ref, sub_ref, send_ref, slot_ref, *, loop_count, capacity, devices, tiled
):
    rows, width = emb_ref.shape
    slots = devices * capacity
    owner = owner_ref[...]
    sub = sub_ref[...]
    dest = sub % loop_count * (devices // loop_count) + owner
    onehot_t = (lax.broadcasted_iota(jnp.int32, (devices, rows), 0) == dest).astype(jnp.bfloat16)
    upper = (
        lax.broadcasted_iota(jnp.int32, (rows, rows), 0)
        < lax.broadcasted_iota(jnp.int32, (rows, rows), 1)
    ).astype(jnp.bfloat16)
    earlier_t = jnp.dot(onehot_t, upper, preferred_element_type=jnp.float32)
    within = jnp.sum(earlier_t * onehot_t.astype(jnp.float32), axis=0, keepdims=True)
    slot = dest * capacity + within.astype(jnp.int32)
    slot_ref[...] = slot
    placing = (lax.broadcasted_iota(jnp.int32, (slots, rows), 0) == slot).astype(jnp.bfloat16)
    placed = jnp.dot(placing, emb_ref[...], preferred_element_type=jnp.float32).astype(
        send_ref.dtype
    )
    if not tiled:
        which = lax.broadcasted_iota(jnp.int32, (LABEL_COLUMNS, rows), 0)
        block = lax.broadcasted_iota(jnp.int32, (LABEL_COLUMNS, rows), 1) // BLOCK
        labels_t = jnp.where(which == 0, block + 1, jnp.where(which == 1, sub + 1, 0))
        labels = labels_t.astype(jnp.float32).T.astype(jnp.bfloat16)
        placed_labels = jnp.dot(placing, labels, preferred_element_type=jnp.float32).astype(
            send_ref.dtype
        )
        send_ref[:, :width] = placed
        send_ref[:, width:] = placed_labels
        return
    row_tiles = capacity // TILE
    col_tiles = width // LABEL_COLUMNS
    which = lax.broadcasted_iota(jnp.int32, (8, rows), 0)
    block = lax.broadcasted_iota(jnp.int32, (8, rows), 1) // BLOCK
    labels_rows = jnp.where(which == 0, block + 1, jnp.where(which == 1, sub + 1, 0))
    placed_rows = lax.dot_general(
        labels_rows.astype(jnp.float32).astype(jnp.bfloat16),
        placing,
        (((1,), (1,)), ((), ())),
        preferred_element_type=jnp.float32,
    ).astype(send_ref.dtype)
    body_rows = row_tiles * col_tiles * TILE
    per_lanes = LABEL_COLUMNS // capacity
    for chunk in range(devices):
        base = chunk * capacity
        for a in range(row_tiles):
            for e in range(col_tiles):
                send_ref[chunk, (a * col_tiles + e) * TILE : (a * col_tiles + e + 1) * TILE, :] = placed[
                    base + a * TILE : base + (a + 1) * TILE, e * LABEL_COLUMNS : (e + 1) * LABEL_COLUMNS
                ]
        lanes = chunk // per_lanes * LABEL_COLUMNS
        send_ref[chunk, body_rows : body_rows + 8, :] = placed_rows[:, lanes : lanes + LABEL_COLUMNS]
        send_ref[chunk, body_rows + 8 :, :] = jnp.zeros((TILE - 8, LABEL_COLUMNS), send_ref.dtype)


def place(emb, row_owner, row_sub, loop_count, capacity, devices, tiled):
    rows, width = emb.shape
    slots = devices * capacity
    vmem = pl.BlockSpec(memory_space=pltpu.VMEM)
    cost = pl.CostEstimate(
        flops=2 * slots * rows * (width + LABEL_COLUMNS) + 2 * devices * rows * rows,
        transcendentals=0,
        bytes_accessed=rows * width * 2 + slots * (width + LABEL_COLUMNS) * 2,
    )
    if tiled:
        shape = (devices, capacity * width // LABEL_COLUMNS + TILE, LABEL_COLUMNS)
    else:
        shape = (slots, width + LABEL_COLUMNS)
    return pl.pallas_call(
        functools.partial(
            place_kernel, loop_count=loop_count, capacity=capacity, devices=devices, tiled=tiled
        ),
        out_shape=(
            jax.ShapeDtypeStruct(shape, jnp.bfloat16),
            jax.ShapeDtypeStruct((1, rows), jnp.int32),
        ),
        in_specs=[vmem] * 3,
        out_specs=(vmem, vmem),
        cost_estimate=cost,
    )(emb, row_owner[None, :], row_sub[None, :])


def attend(keys, near, sub):
    slots = keys.shape[0]
    scale = 4.0 / keys.shape[1]
    scores = scale * lax.dot_general(
        keys, keys, (((1,), (1,)), ((), ())), preferred_element_type=jnp.float32
    )
    index = jnp.arange(slots, dtype=jnp.int32)
    same = (index[:, None] == index[None, :]) | (
        (sub[:, None] == sub[None, :]) & near
    )
    top = jnp.max(jnp.where(same, scores, jnp.float32(-1e30)), axis=1)
    weights = jnp.where(same, jnp.exp(scores - top[:, None]), jnp.float32(0.0))
    total = jnp.sum(weights, axis=1)
    summed = jnp.dot(weights.astype(jnp.bfloat16), keys, preferred_element_type=jnp.float32)
    return (summed * (1.0 / total)[:, None]).astype(jnp.bfloat16)


def body(emb, row_owner, row_sub, cand):
    rows = emb.shape[0]
    owner_count = lax.axis_size("owner")
    loop_count = lax.axis_size("loop")
    devices = owner_count * loop_count
    capacity = 2 * rows // owner_count // loop_count
    slots = devices * capacity
    local_blocks = rows // BLOCK
    axes = ("loop", "owner")

    width = emb.shape[1]
    tiled = capacity % TILE == 0 and width % LABEL_COLUMNS == 0 and LABEL_COLUMNS % capacity == 0
    send, slot_of_row = place(emb, row_owner, row_sub, loop_count, capacity, devices, tiled)
    slot_of_row = slot_of_row[0]
    gathering = (slot_of_row[:, None] == jnp.arange(slots, dtype=jnp.int32)[None, :]).astype(
        jnp.bfloat16
    )
    held = lax.all_to_all(send, axes, split_axis=0, concat_axis=0, tiled=True)
    if tiled:
        row_tiles = capacity // TILE
        col_tiles = width // LABEL_COLUMNS
        body_rows = row_tiles * col_tiles * TILE
        held_emb = held[:, :body_rows].reshape(devices, row_tiles, col_tiles, TILE, LABEL_COLUMNS)
        held_emb = held_emb.transpose(0, 1, 3, 2, 4).reshape(slots, width)
        per_lanes = LABEL_COLUMNS // capacity
        lanes = held[:, body_rows : body_rows + 2, :].reshape(devices, 2, per_lanes, capacity)
        me = lax.axis_index("loop") * owner_count + lax.axis_index("owner")
        held_labels = lax.dynamic_index_in_dim(lanes, me % per_lanes, axis=2, keepdims=False)
        held_labels = held_labels.astype(jnp.int32).transpose(0, 2, 1).reshape(slots, 2)
    else:
        held_emb = held[:, :width]
        held_labels = held[:, width : width + 2].astype(jnp.int32)

    index = jnp.arange(slots, dtype=jnp.int32)
    present = held_labels[:, 0] > 0
    source = index // capacity
    source = source % owner_count * loop_count + source // owner_count
    global_block = source * local_blocks + held_labels[:, 0] - 1
    global_block = jnp.where(present, global_block, 0)
    sub = jnp.where(present, held_labels[:, 1] - 1, -1 - index)
    block_count = cand.shape[1]
    block_onehot = (
        global_block[:, None] == jnp.arange(block_count, dtype=jnp.int32)[None, :]
    ).astype(jnp.bfloat16)
    cand_rows = jnp.dot(block_onehot, cand.astype(jnp.bfloat16), preferred_element_type=jnp.float32)
    near = (
        lax.dot_general(
            cand_rows.astype(jnp.bfloat16),
            block_onehot,
            (((1,), (1,)), ((), ())),
            preferred_element_type=jnp.float32,
        )
        > 0.5
    )
    averaged = attend(held_emb, near, sub)
    returned = lax.all_to_all(averaged, axes, split_axis=0, concat_axis=0, tiled=True)
    result = jnp.dot(gathering, returned, preferred_element_type=jnp.float32)
    return result.astype(jnp.bfloat16)


def solution(mesh):
    return jax.shard_map(
        body,
        mesh=mesh,
        in_specs=(
            P(("groups", "owner", "loop"), None),
            P(("groups", "owner", "loop")),
            P(("groups", "owner", "loop")),
            P("groups", None),
        ),
        out_specs=P(("groups", "owner", "loop"), None),
        check_vma=False,
    )
```

```python
import functools

import jax
import jax.numpy as jnp
from jax import lax
from jax.experimental import pallas as pl
from jax.experimental.pallas import tpu as pltpu
from jax.sharding import PartitionSpec as P

BLOCK = 128
SUB = 16
LABEL_COLUMNS = 128
TILE = 16


def place_kernel(
    emb_ref, owner_ref, sub_ref, send_ref, slot_ref, *, loop_count, capacity, devices, tiled
):
    rows, width = emb_ref.shape
    slots = devices * capacity
    owner = owner_ref[...]
    sub = sub_ref[...]
    dest = sub % loop_count * (devices // loop_count) + owner
    onehot_t = (lax.broadcasted_iota(jnp.int32, (devices, rows), 0) == dest).astype(jnp.bfloat16)
    upper = (
        lax.broadcasted_iota(jnp.int32, (rows, rows), 0)
        < lax.broadcasted_iota(jnp.int32, (rows, rows), 1)
    ).astype(jnp.bfloat16)
    earlier_t = jnp.dot(onehot_t, upper, preferred_element_type=jnp.float32)
    within = jnp.sum(earlier_t * onehot_t.astype(jnp.float32), axis=0, keepdims=True)
    slot = dest * capacity + within.astype(jnp.int32)
    slot_ref[...] = slot
    placing = (lax.broadcasted_iota(jnp.int32, (slots, rows), 0) == slot).astype(jnp.bfloat16)
    placed = jnp.dot(placing, emb_ref[...], preferred_element_type=jnp.float32).astype(
        send_ref.dtype
    )
    if not tiled:
        which = lax.broadcasted_iota(jnp.int32, (LABEL_COLUMNS, rows), 0)
        block = lax.broadcasted_iota(jnp.int32, (LABEL_COLUMNS, rows), 1) // BLOCK
        labels_t = jnp.where(which == 0, block + 1, jnp.where(which == 1, sub + 1, 0))
        labels = labels_t.astype(jnp.float32).T.astype(jnp.bfloat16)
        placed_labels = jnp.dot(placing, labels, preferred_element_type=jnp.float32).astype(
            send_ref.dtype
        )
        send_ref[:, :width] = placed
        send_ref[:, width:] = placed_labels
        return
    row_tiles = capacity // TILE
    col_tiles = width // LABEL_COLUMNS
    which = lax.broadcasted_iota(jnp.int32, (8, rows), 0)
    block = lax.broadcasted_iota(jnp.int32, (8, rows), 1) // BLOCK
    labels_rows = jnp.where(which == 0, block + 1, jnp.where(which == 1, sub + 1, 0))
    placed_rows = lax.dot_general(
        labels_rows.astype(jnp.float32).astype(jnp.bfloat16),
        placing,
        (((1,), (1,)), ((), ())),
        preferred_element_type=jnp.float32,
    ).astype(send_ref.dtype)
    body_rows = row_tiles * col_tiles * TILE
    per_lanes = LABEL_COLUMNS // capacity
    for chunk in range(devices):
        base = chunk * capacity
        for a in range(row_tiles):
            for e in range(col_tiles):
                send_ref[chunk, (a * col_tiles + e) * TILE : (a * col_tiles + e + 1) * TILE, :] = placed[
                    base + a * TILE : base + (a + 1) * TILE, e * LABEL_COLUMNS : (e + 1) * LABEL_COLUMNS
                ]
        lanes = chunk // per_lanes * LABEL_COLUMNS
        send_ref[chunk, body_rows : body_rows + 8, :] = placed_rows[:, lanes : lanes + LABEL_COLUMNS]
        send_ref[chunk, body_rows + 8 :, :] = jnp.zeros((TILE - 8, LABEL_COLUMNS), send_ref.dtype)


def place(emb, row_owner, row_sub, loop_count, capacity, devices, tiled):
    rows, width = emb.shape
    slots = devices * capacity
    vmem = pl.BlockSpec(memory_space=pltpu.VMEM)
    cost = pl.CostEstimate(
        flops=2 * slots * rows * (width + LABEL_COLUMNS) + 2 * devices * rows * rows,
        transcendentals=0,
        bytes_accessed=rows * width * 2 + slots * (width + LABEL_COLUMNS) * 2,
    )
    if tiled:
        shape = (devices, capacity * width // LABEL_COLUMNS + TILE, LABEL_COLUMNS)
    else:
        shape = (slots, width + LABEL_COLUMNS)
    return pl.pallas_call(
        functools.partial(
            place_kernel, loop_count=loop_count, capacity=capacity, devices=devices, tiled=tiled
        ),
        out_shape=(
            jax.ShapeDtypeStruct(shape, jnp.bfloat16),
            jax.ShapeDtypeStruct((1, rows), jnp.int32),
        ),
        in_specs=[vmem] * 3,
        out_specs=(vmem, vmem),
        cost_estimate=cost,
    )(emb, row_owner[None, :], row_sub[None, :])


def attend(keys, near, sub):
    slots = keys.shape[0]
    scale = 4.0 / keys.shape[1]
    scores = scale * lax.dot_general(
        keys, keys, (((1,), (1,)), ((), ())), preferred_element_type=jnp.float32
    )
    index = jnp.arange(slots, dtype=jnp.int32)
    same = (index[:, None] == index[None, :]) | (
        (sub[:, None] == sub[None, :]) & near
    )
    top = jnp.max(jnp.where(same, scores, jnp.float32(-1e30)), axis=1)
    weights = jnp.where(same, jnp.exp(scores - top[:, None]), jnp.float32(0.0))
    total = jnp.sum(weights, axis=1)
    summed = jnp.dot(weights.astype(jnp.bfloat16), keys, preferred_element_type=jnp.float32)
    return (summed / total[:, None]).astype(jnp.bfloat16)


def body(emb, row_owner, row_sub, cand):
    rows = emb.shape[0]
    owner_count = lax.axis_size("owner")
    loop_count = lax.axis_size("loop")
    devices = owner_count * loop_count
    capacity = 2 * rows // owner_count // loop_count
    slots = devices * capacity
    local_blocks = rows // BLOCK
    axes = ("loop", "owner")

    width = emb.shape[1]
    tiled = capacity % TILE == 0 and width % LABEL_COLUMNS == 0 and LABEL_COLUMNS % capacity == 0
    send, slot_of_row = place(emb, row_owner, row_sub, loop_count, capacity, devices, tiled)
    slot_of_row = slot_of_row[0]
    pair_slot = slot_of_row[::2] // 2
    gathering = (pair_slot[:, None] == jnp.arange(slots // 2, dtype=jnp.int32)[None, :]).astype(
        jnp.bfloat16
    )
    held = lax.all_to_all(send, axes, split_axis=0, concat_axis=0, tiled=True)
    if tiled:
        row_tiles = capacity // TILE
        col_tiles = width // LABEL_COLUMNS
        body_rows = row_tiles * col_tiles * TILE
        held_emb = held[:, :body_rows].reshape(devices, row_tiles, col_tiles, TILE, LABEL_COLUMNS)
        held_emb = held_emb.transpose(0, 1, 3, 2, 4).reshape(slots, width)
        per_lanes = LABEL_COLUMNS // capacity
        lanes = held[:, body_rows : body_rows + 2, :].reshape(devices, 2, per_lanes, capacity)
        me = lax.axis_index("loop") * owner_count + lax.axis_index("owner")
        held_labels = lax.dynamic_index_in_dim(lanes, me % per_lanes, axis=2, keepdims=False)
        held_labels = held_labels.astype(jnp.int32).transpose(0, 2, 1).reshape(slots, 2)
    else:
        held_emb = held[:, :width]
        held_labels = held[:, width : width + 2].astype(jnp.int32)

    index = jnp.arange(slots, dtype=jnp.int32)
    present = held_labels[:, 0] > 0
    source = index // capacity
    source = source % owner_count * loop_count + source // owner_count
    global_block = source * local_blocks + held_labels[:, 0] - 1
    global_block = jnp.where(present, global_block, 0)
    sub = jnp.where(present, held_labels[:, 1] - 1, -1 - index)
    block_count = cand.shape[1]
    block_onehot = (
        global_block[:, None] == jnp.arange(block_count, dtype=jnp.int32)[None, :]
    ).astype(jnp.bfloat16)
    cand_rows = jnp.dot(block_onehot, cand.astype(jnp.bfloat16), preferred_element_type=jnp.float32)
    near = (
        lax.dot_general(
            cand_rows.astype(jnp.bfloat16),
            block_onehot,
            (((1,), (1,)), ((), ())),
            preferred_element_type=jnp.float32,
        )
        > 0.5
    )
    averaged = attend(held_emb, near, sub)
    returned = lax.all_to_all(averaged, axes, split_axis=0, concat_axis=0, tiled=True)
    result = jnp.dot(
        gathering, returned.reshape(slots // 2, 2 * width), preferred_element_type=jnp.float32
    ).reshape(rows, width)
    return result.astype(jnp.bfloat16)


def solution(mesh):
    return jax.shard_map(
        body,
        mesh=mesh,
        in_specs=(
            P(("groups", "owner", "loop"), None),
            P(("groups", "owner", "loop")),
            P(("groups", "owner", "loop")),
            P("groups", None),
        ),
        out_specs=P(("groups", "owner", "loop"), None),
        check_vma=False,
    )
```

```python
import functools

import jax
import jax.numpy as jnp
from jax import lax
from jax.experimental import pallas as pl
from jax.experimental.pallas import tpu as pltpu
from jax.sharding import PartitionSpec as P

BLOCK = 128
SUB = 16
LABEL_COLUMNS = 128
TILE = 16


def place_kernel(
    emb_ref, owner_ref, sub_ref, send_ref, slot_ref, *, loop_count, capacity, devices, tiled
):
    rows, width = emb_ref.shape
    slots = devices * capacity
    owner = owner_ref[...]
    sub = sub_ref[...]
    dest = sub % loop_count * (devices // loop_count) + owner
    onehot_t = (lax.broadcasted_iota(jnp.int32, (devices, rows), 0) == dest).astype(jnp.bfloat16)
    upper = (
        lax.broadcasted_iota(jnp.int32, (rows, rows), 0)
        < lax.broadcasted_iota(jnp.int32, (rows, rows), 1)
    ).astype(jnp.bfloat16)
    earlier_t = jnp.dot(onehot_t, upper, preferred_element_type=jnp.float32)
    within = jnp.sum(earlier_t * onehot_t.astype(jnp.float32), axis=0, keepdims=True)
    slot = dest * capacity + within.astype(jnp.int32)
    slot_ref[...] = slot
    placing = (lax.broadcasted_iota(jnp.int32, (slots, rows), 0) == slot).astype(jnp.bfloat16)
    placed = jnp.dot(placing, emb_ref[...], preferred_element_type=jnp.float32).astype(
        send_ref.dtype
    )
    if not tiled:
        which = lax.broadcasted_iota(jnp.int32, (LABEL_COLUMNS, rows), 0)
        block = lax.broadcasted_iota(jnp.int32, (LABEL_COLUMNS, rows), 1) // BLOCK
        labels_t = jnp.where(which == 0, block + 1, jnp.where(which == 1, sub + 1, 0))
        labels = labels_t.astype(jnp.float32).T.astype(jnp.bfloat16)
        placed_labels = jnp.dot(placing, labels, preferred_element_type=jnp.float32).astype(
            send_ref.dtype
        )
        send_ref[:, :width] = placed
        send_ref[:, width:] = placed_labels
        return
    row_tiles = capacity // TILE
    col_tiles = width // LABEL_COLUMNS
    which = lax.broadcasted_iota(jnp.int32, (8, rows), 0)
    block = lax.broadcasted_iota(jnp.int32, (8, rows), 1) // BLOCK
    labels_rows = jnp.where(which == 0, block + 1, jnp.where(which == 1, sub + 1, 0))
    placed_rows = lax.dot_general(
        labels_rows.astype(jnp.float32).astype(jnp.bfloat16),
        placing,
        (((1,), (1,)), ((), ())),
        preferred_element_type=jnp.float32,
    ).astype(send_ref.dtype)
    body_rows = row_tiles * col_tiles * TILE
    per_lanes = LABEL_COLUMNS // capacity
    for chunk in range(devices):
        base = chunk * capacity
        for a in range(row_tiles):
            for e in range(col_tiles):
                send_ref[chunk, (a * col_tiles + e) * TILE : (a * col_tiles + e + 1) * TILE, :] = placed[
                    base + a * TILE : base + (a + 1) * TILE, e * LABEL_COLUMNS : (e + 1) * LABEL_COLUMNS
                ]
        lanes = chunk // per_lanes * LABEL_COLUMNS
        send_ref[chunk, body_rows : body_rows + 8, :] = placed_rows[:, lanes : lanes + LABEL_COLUMNS]
        send_ref[chunk, body_rows + 8 :, :] = jnp.zeros((TILE - 8, LABEL_COLUMNS), send_ref.dtype)


def place(emb, row_owner, row_sub, loop_count, capacity, devices, tiled):
    rows, width = emb.shape
    slots = devices * capacity
    vmem = pl.BlockSpec(memory_space=pltpu.VMEM)
    cost = pl.CostEstimate(
        flops=2 * slots * rows * (width + LABEL_COLUMNS) + 2 * devices * rows * rows,
        transcendentals=0,
        bytes_accessed=rows * width * 2 + slots * (width + LABEL_COLUMNS) * 2,
    )
    if tiled:
        shape = (devices, capacity * width // LABEL_COLUMNS + TILE, LABEL_COLUMNS)
    else:
        shape = (slots, width + LABEL_COLUMNS)
    return pl.pallas_call(
        functools.partial(
            place_kernel, loop_count=loop_count, capacity=capacity, devices=devices, tiled=tiled
        ),
        out_shape=(
            jax.ShapeDtypeStruct(shape, jnp.bfloat16),
            jax.ShapeDtypeStruct((1, rows), jnp.int32),
        ),
        in_specs=[vmem] * 3,
        out_specs=(vmem, vmem),
        cost_estimate=cost,
    )(emb, row_owner[None, :], row_sub[None, :])


def attend(keys, near, sub):
    slots = keys.shape[0]
    scale = 4.0 / keys.shape[1]
    scores = scale * lax.dot_general(
        keys, keys, (((1,), (1,)), ((), ())), preferred_element_type=jnp.float32
    )
    index = jnp.arange(slots, dtype=jnp.int32)
    same = (index[:, None] == index[None, :]) | (
        (sub[:, None] == sub[None, :]) & near
    )
    top = jnp.max(jnp.where(same, scores, jnp.float32(-1e30)), axis=1)
    weights = jnp.where(same, jnp.exp(scores - top[:, None]), jnp.float32(0.0))
    total = jnp.sum(weights, axis=1)
    summed = jnp.dot(weights.astype(jnp.bfloat16), keys, preferred_element_type=jnp.float32)
    return (summed / total[:, None]).astype(jnp.bfloat16)


def body(emb, row_owner, row_sub, cand):
    rows = emb.shape[0]
    owner_count = lax.axis_size("owner")
    loop_count = lax.axis_size("loop")
    devices = owner_count * loop_count
    capacity = 2 * rows // owner_count // loop_count
    slots = devices * capacity
    local_blocks = rows // BLOCK
    axes = ("loop", "owner")

    width = emb.shape[1]
    tiled = capacity % TILE == 0 and width % LABEL_COLUMNS == 0 and LABEL_COLUMNS % capacity == 0
    send, slot_of_row = place(emb, row_owner, row_sub, loop_count, capacity, devices, tiled)
    slot_of_row = slot_of_row[0]
    gathering = (slot_of_row[:, None] == jnp.arange(slots, dtype=jnp.int32)[None, :]).astype(
        jnp.bfloat16
    )
    held = lax.all_to_all(send, axes, split_axis=0, concat_axis=0, tiled=True)
    if tiled:
        row_tiles = capacity // TILE
        col_tiles = width // LABEL_COLUMNS
        body_rows = row_tiles * col_tiles * TILE
        held_emb = held[:, :body_rows].reshape(devices, row_tiles, col_tiles, TILE, LABEL_COLUMNS)
        held_emb = held_emb.transpose(0, 1, 3, 2, 4).reshape(slots, width)
        per_lanes = LABEL_COLUMNS // capacity
        lanes = held[:, body_rows : body_rows + 2, :].reshape(devices, 2, per_lanes, capacity)
        me = lax.axis_index("loop") * owner_count + lax.axis_index("owner")
        held_labels = lax.dynamic_index_in_dim(lanes, me % per_lanes, axis=2, keepdims=False)
        held_labels = held_labels.astype(jnp.int32).transpose(0, 2, 1).reshape(slots, 2)
    else:
        held_emb = held[:, :width]
        held_labels = held[:, width : width + 2].astype(jnp.int32)

    index = jnp.arange(slots, dtype=jnp.int32)
    present = held_labels[:, 0] > 0
    source = index // capacity
    source = source % owner_count * loop_count + source // owner_count
    global_block = source * local_blocks + held_labels[:, 0] - 1
    global_block = jnp.where(present, global_block, 0)
    sub = jnp.where(present, held_labels[:, 1] - 1, -1 - index)
    block_count = cand.shape[1]
    block_onehot = (
        global_block[:, None] == jnp.arange(block_count, dtype=jnp.int32)[None, :]
    ).astype(jnp.bfloat16)
    cand_rows = jnp.dot(block_onehot, cand.astype(jnp.bfloat16), preferred_element_type=jnp.float32)
    block_onehot_t = (
        jnp.arange(block_count, dtype=jnp.int32)[:, None] == global_block[None, :]
    ).astype(jnp.bfloat16)
    near = (
        jnp.dot(cand_rows.astype(jnp.bfloat16), block_onehot_t, preferred_element_type=jnp.float32)
        > 0.5
    )
    averaged = attend(held_emb, near, sub)
    returned = lax.all_to_all(averaged, axes, split_axis=0, concat_axis=0, tiled=True)
    result = jnp.dot(gathering, returned, preferred_element_type=jnp.float32)
    return result.astype(jnp.bfloat16)


def solution(mesh):
    return jax.shard_map(
        body,
        mesh=mesh,
        in_specs=(
            P(("groups", "owner", "loop"), None),
            P(("groups", "owner", "loop")),
            P(("groups", "owner", "loop")),
            P("groups", None),
        ),
        out_specs=P(("groups", "owner", "loop"), None),
        check_vma=False,
    )
```

```python
import functools

import jax
import jax.numpy as jnp
from jax import lax
from jax.experimental import pallas as pl
from jax.experimental.pallas import tpu as pltpu
from jax.sharding import PartitionSpec as P

BLOCK = 128
SUB = 16
LABEL_COLUMNS = 128
TILE = 16


def place_kernel(
    emb_ref, owner_ref, sub_ref, send_ref, slot_ref, *, loop_count, capacity, devices, tiled
):
    rows, width = emb_ref.shape
    slots = devices * capacity
    owner = owner_ref[...]
    sub = sub_ref[...]
    dest = sub % loop_count * (devices // loop_count) + owner
    onehot_t = (lax.broadcasted_iota(jnp.int32, (devices, rows), 0) == dest).astype(jnp.bfloat16)
    upper = (
        lax.broadcasted_iota(jnp.int32, (rows, rows), 0)
        < lax.broadcasted_iota(jnp.int32, (rows, rows), 1)
    ).astype(jnp.bfloat16)
    earlier_t = jnp.dot(onehot_t, upper, preferred_element_type=jnp.float32)
    within = jnp.sum(earlier_t * onehot_t.astype(jnp.float32), axis=0, keepdims=True)
    slot = dest * capacity + within.astype(jnp.int32)
    slot_ref[...] = slot
    placing = (lax.broadcasted_iota(jnp.int32, (slots, rows), 0) == slot).astype(jnp.bfloat16)
    placed = jnp.dot(placing, emb_ref[...], preferred_element_type=jnp.float32).astype(
        send_ref.dtype
    )
    if not tiled:
        which = lax.broadcasted_iota(jnp.int32, (LABEL_COLUMNS, rows), 0)
        block = lax.broadcasted_iota(jnp.int32, (LABEL_COLUMNS, rows), 1) // BLOCK
        labels_t = jnp.where(which == 0, block + 1, jnp.where(which == 1, sub + 1, 0))
        labels = labels_t.astype(jnp.float32).T.astype(jnp.bfloat16)
        placed_labels = jnp.dot(placing, labels, preferred_element_type=jnp.float32).astype(
            send_ref.dtype
        )
        send_ref[:, :width] = placed
        send_ref[:, width:] = placed_labels
        return
    row_tiles = capacity // TILE
    col_tiles = width // LABEL_COLUMNS
    which = lax.broadcasted_iota(jnp.int32, (8, rows), 0)
    block = lax.broadcasted_iota(jnp.int32, (8, rows), 1) // BLOCK
    labels_rows = jnp.where(which == 0, block + 1, jnp.where(which == 1, sub + 1, 0))
    placed_rows = lax.dot_general(
        labels_rows.astype(jnp.float32).astype(jnp.bfloat16),
        placing,
        (((1,), (1,)), ((), ())),
        preferred_element_type=jnp.float32,
    )
    body_rows = row_tiles * col_tiles * TILE
    for chunk in range(devices):
        base = chunk * capacity
        for a in range(row_tiles):
            for e in range(col_tiles):
                send_ref[chunk, (a * col_tiles + e) * TILE : (a * col_tiles + e + 1) * TILE, :] = placed[
                    base + a * TILE : base + (a + 1) * TILE, e * LABEL_COLUMNS : (e + 1) * LABEL_COLUMNS
                ]
        rolled = placed_rows
        if chunk:
            rolled = pltpu.roll(placed_rows, slots - base, 1)
        send_ref[chunk, body_rows : body_rows + 8, :] = rolled[:, :LABEL_COLUMNS].astype(
            send_ref.dtype
        )
        send_ref[chunk, body_rows + 8 :, :] = jnp.zeros((TILE - 8, LABEL_COLUMNS), send_ref.dtype)


def place(emb, row_owner, row_sub, loop_count, capacity, devices, tiled):
    rows, width = emb.shape
    slots = devices * capacity
    vmem = pl.BlockSpec(memory_space=pltpu.VMEM)
    cost = pl.CostEstimate(
        flops=2 * slots * rows * (width + LABEL_COLUMNS) + 2 * devices * rows * rows,
        transcendentals=0,
        bytes_accessed=rows * width * 2 + slots * (width + LABEL_COLUMNS) * 2,
    )
    if tiled:
        shape = (devices, capacity * width // LABEL_COLUMNS + TILE, LABEL_COLUMNS)
    else:
        shape = (slots, width + LABEL_COLUMNS)
    return pl.pallas_call(
        functools.partial(
            place_kernel, loop_count=loop_count, capacity=capacity, devices=devices, tiled=tiled
        ),
        out_shape=(
            jax.ShapeDtypeStruct(shape, jnp.bfloat16),
            jax.ShapeDtypeStruct((1, rows), jnp.int32),
        ),
        in_specs=[vmem] * 3,
        out_specs=(vmem, vmem),
        cost_estimate=cost,
    )(emb, row_owner[None, :], row_sub[None, :])


def attend(keys, near, sub):
    slots = keys.shape[0]
    scale = 4.0 / keys.shape[1]
    scores = scale * lax.dot_general(
        keys, keys, (((1,), (1,)), ((), ())), preferred_element_type=jnp.float32
    )
    index = jnp.arange(slots, dtype=jnp.int32)
    same = (index[:, None] == index[None, :]) | (
        (sub[:, None] == sub[None, :]) & near
    )
    top = jnp.max(jnp.where(same, scores, jnp.float32(-1e30)), axis=1)
    weights = jnp.where(same, jnp.exp(scores - top[:, None]), jnp.float32(0.0))
    total = jnp.sum(weights, axis=1)
    summed = jnp.dot(weights.astype(jnp.bfloat16), keys, preferred_element_type=jnp.float32)
    return (summed / total[:, None]).astype(jnp.bfloat16)


def body(emb, row_owner, row_sub, cand):
    rows = emb.shape[0]
    owner_count = lax.axis_size("owner")
    loop_count = lax.axis_size("loop")
    devices = owner_count * loop_count
    capacity = 2 * rows // owner_count // loop_count
    slots = devices * capacity
    local_blocks = rows // BLOCK
    axes = ("loop", "owner")

    width = emb.shape[1]
    tiled = capacity % TILE == 0 and width % LABEL_COLUMNS == 0 and LABEL_COLUMNS % capacity == 0
    send, slot_of_row = place(emb, row_owner, row_sub, loop_count, capacity, devices, tiled)
    slot_of_row = slot_of_row[0]
    gathering = (slot_of_row[:, None] == jnp.arange(slots, dtype=jnp.int32)[None, :]).astype(
        jnp.bfloat16
    )
    held = lax.all_to_all(send, axes, split_axis=0, concat_axis=0, tiled=True)
    if tiled:
        row_tiles = capacity // TILE
        col_tiles = width // LABEL_COLUMNS
        body_rows = row_tiles * col_tiles * TILE
        held_emb = held[:, :body_rows].reshape(devices, row_tiles, col_tiles, TILE, LABEL_COLUMNS)
        held_emb = held_emb.transpose(0, 1, 3, 2, 4).reshape(slots, width)
        held_labels = held[:, body_rows : body_rows + 2, :capacity]
        held_labels = held_labels.astype(jnp.int32).transpose(0, 2, 1).reshape(slots, 2)
    else:
        held_emb = held[:, :width]
        held_labels = held[:, width : width + 2].astype(jnp.int32)

    index = jnp.arange(slots, dtype=jnp.int32)
    present = held_labels[:, 0] > 0
    source = index // capacity
    source = source % owner_count * loop_count + source // owner_count
    global_block = source * local_blocks + held_labels[:, 0] - 1
    global_block = jnp.where(present, global_block, 0)
    sub = jnp.where(present, held_labels[:, 1] - 1, -1 - index)
    block_count = cand.shape[1]
    block_onehot = (
        global_block[:, None] == jnp.arange(block_count, dtype=jnp.int32)[None, :]
    ).astype(jnp.bfloat16)
    cand_rows = jnp.dot(block_onehot, cand.astype(jnp.bfloat16), preferred_element_type=jnp.float32)
    near = (
        lax.dot_general(
            cand_rows.astype(jnp.bfloat16),
            block_onehot,
            (((1,), (1,)), ((), ())),
            preferred_element_type=jnp.float32,
        )
        > 0.5
    )
    averaged = attend(held_emb, near, sub)
    returned = lax.all_to_all(averaged, axes, split_axis=0, concat_axis=0, tiled=True)
    result = jnp.dot(gathering, returned, preferred_element_type=jnp.float32)
    return result.astype(jnp.bfloat16)


def solution(mesh):
    return jax.shard_map(
        body,
        mesh=mesh,
        in_specs=(
            P(("groups", "owner", "loop"), None),
            P(("groups", "owner", "loop")),
            P(("groups", "owner", "loop")),
            P("groups", None),
        ),
        out_specs=P(("groups", "owner", "loop"), None),
        check_vma=False,
    )
```
